256 devices in a mesh: dp: 64 (over z, x, core), mp: 4 (over y).
Axes of the slice: x: 4, y: 4, z: 8, core: 2. Of those that a mesh axis runs over, the one named last changes fastest.
Arguments:
- embed_table: float32 [16, 32768, 256], P('mp', 'dp'), may hold values from -5 to 5
- accum: float32 [16, 32768], P('mp', 'dp'), may hold values from 0.1 to 3
- stale_grad: bfloat16 [16, 32768, 256], P('mp', 'dp'), may hold values from -6 to 6
- grad_owner: int32 [16, 32768, 1], P('mp', 'dp'), may hold values from 0 to 63; in each aligned block of 512 rows (0 to 511, 512 to 1023, ..., all dimensions but the last counted through in order) at most 16 rows name the same one
- grad_row: int32 [16, 32768], P('mp', 'dp'), may hold values from 0 to 511
- lookup_owner: int32 [16, 32768, 1], P('mp', 'dp'), may hold values from 0 to 63; in each aligned block of 512 rows (0 to 511, 512 to 1023, ..., all dimensions but the last counted through in order) at most 16 rows name the same one
- lookup_row: int32 [16, 32768], P('mp', 'dp'), may hold values from 0 to 511
- bag_len: int32 [16, 16384], P('mp', 'dp'), may hold values from 1 to 2
- label: int32 [16384], P('dp'), may hold values 0 or 1
- up_factor_weight: bfloat16 [2, 512, 4096], P(None, None, 'mp'), may hold values from -0.25 to 0.25
- v_weight: bfloat16 [2, 512, 4096], P(None, None, 'mp'), may hold values from -0.09375 to 0.09375
- cross_bias: float32 [2, 4096], P(None, 'mp'), may hold values from -3 to 3
- head_weight: float32 [4096], P('mp'), may hold values from -0.09375 to 0.09375
Outputs:
- new_table: float32 [16, 32768, 256], P('mp', 'dp')
- new_accum: float32 [16, 32768], P('mp', 'dp')
- grad_u: float32 [2, 512, 4096], P(None, 'dp', 'mp')
- grad_v: float32 [2, 512, 4096], P(None, 'dp', 'mp')
- grad_small: float32 [3, 4096], P(None, 'mp')
- grad_pooled: bfloat16 [16384, 4096], P('dp', 'mp')
The draws below stay inside these ranges and needn't reach their ends.
Inputs may be any that keep to these rules, and one draw needn't show every extreme that they name: `grad_owner`: among the 512 blocks of one feature held by one index of dp, at most 16 name the same owner, and in some such group exactly 16 do. `lookup_owner`: among the 512 id slots of one feature belonging to one index of dp, at most 16 name the same owner, and in some such group exactly 16 do; slots k >= bag_len are unused.
All inputs are finite; a program needn't handle non-finite values. No bound on the sum of `label` on one device may be relied on, other than what follows from the above.
Results may differ from the reference program's by a relative error of at most 0.009.
Values may be sent and summed in bfloat16 or wider, within the bound.
No kernel may reach another device: no remote copies, remote signals or barrier semaphores. Data moves between devices by JAX's collectives and lax.ppermute only.
A program may use at most 128 MiB of HBM per device.

```python
import math
import jax
import jax.numpy as jnp
import numpy as np
from jax import lax

E = 256
F = 16
R = 512
LC = 2
BAG = 2
B_DEV = 256
ROWS_DEV = 512
GR_DEV = 512
D0 = 4096
BATCH = 16384
ROWS = 32768
GR = 32768
LOOK = 32768
GCAP = 16
LCAP = 16
N_DP = 64


def plant(entries, key, least, high):
    dims = entries.shape
    spot = [jax.random.randint(jax.random.fold_in(key, axis), (), 0, dims[axis]) for axis in range(len(dims))]
    entries = entries.at[tuple(spot)].set(least)
    longest = dims.index(max(dims))
    spot[longest] = (spot[longest] + 1) % dims[longest]
    return entries.at[tuple(spot)].set(high)


def level_of(key, extent, split, least, top_value):
    gain, own = 1.0, jax.random.fold_in(key, 6)
    for dim, shards_of in split:
        draws = jnp.exp(jax.random.uniform(jax.random.fold_in(own, dim), (shards_of,), jnp.float32, least / len(split), top_value / len(split)))
        gain = gain * jnp.repeat(draws, extent[dim] // shards_of).reshape([-1 if axis == dim else 1 for axis in range(len(extent))])
    return gain


def rank_table(amount, lean):
    weights = [(1 << 20) // math.isqrt(grade ** lean) + 1 for grade in range(1, amount + 1)]
    deviation = 1 + sum(weights) // (1 << 30)
    return np.cumsum(np.array([max(1, weight // deviation) for weight in weights]))


def ranked(own_key, shape, count, lean):
    grid = rank_table(count, lean)
    pick = jax.random.randint(jax.random.fold_in(own_key, 1), shape, 0, int(grid[count - 1]))
    grade = jnp.searchsorted(jnp.asarray(grid, jnp.int32), pick, side="right")
    return jax.random.permutation(jax.random.fold_in(own_key, 2), count)[grade].astype(jnp.int32)


def deal_out(stream_key, own, number, rows, count, top, bound, skew):
    order = jax.random.permutation(stream_key, count)
    crowded, ordinary = shares(count, rows * top, bound, skew, True), shares(count, rows * top, bound, skew, False)
    places = jnp.arange(count)

    def named(tallies, rotation):
        used = int((tallies > 0).sum())
        fixed = max(1, used // 4)
        shifted = fixed + (places - fixed + rotation * (used - fixed)) % max(1, count - fixed)
        return jnp.zeros((count,), jnp.int32).at[order[jnp.where(places < fixed, places, shifted)]].set(jnp.asarray(tallies, jnp.int32))

    tallies = jnp.where(number % 4 == 0, named(crowded, number // 4), named(ordinary, number - number // 4 - 1))
    mixed = jax.random.permutation(jax.random.fold_in(own, 3), count)
    donor, taker = mixed[0:count // 2 * 2:2], mixed[1:count // 2 * 2:2]
    room = jnp.minimum(tallies[donor] - 1, bound - tallies[taker]) // 2
    room = jnp.where((donor == order[0]) | (taker == order[0]) | (tallies[taker] == 0), 0, jnp.maximum(room, 0))
    shifted = jax.random.randint(jax.random.fold_in(own, 4), (count // 2,), 0, 1 << 20) % (room + 1)
    tallies = tallies.at[donor].add(-shifted).at[taker].add(shifted)
    labels = jnp.searchsorted(jnp.cumsum(tallies), jnp.arange(rows * top), side="right").astype(jnp.int32)
    grid = labels.reshape(top, rows).T
    grid = grid[jax.random.permutation(jax.random.fold_in(own, 1), rows)]
    rotation = jax.random.randint(jax.random.fold_in(own, 2), (rows, 1), 0, top)
    return jnp.take_along_axis(grid, (jnp.arange(top)[None, :] + rotation) % top, axis=1)


def shares(amount, total, limit, skew, full):
    weights = [(1 << 20) // math.isqrt(grade ** skew) + 1 for grade in range(1, amount + 1)]
    largest = limit if full else min(limit, max(-(-total // amount), total * weights[0] // sum(weights)))
    least = 1 if total - largest >= amount - 1 else 0
    holding, surplus = [largest] + [least] * (amount - 1), total - largest - least * (amount - 1)
    while surplus > 0:
        movable = [i for i in range(1, amount) if holding[i] < largest] or [i for i in range(1, amount) if holding[i] < limit]
        pool, remaining = sum([weights[i] for i in movable]), surplus
        for i in movable:
            more = min(limit - holding[i], max(1, remaining * weights[i] // pool), surplus)
            holding[i] = holding[i] + more
            surplus = surplus - more
    return np.array(holding)


def noise(key, dims, width, most, shards=(), kind=jnp.bfloat16):
    result = jax.random.normal(key, dims, jnp.float32) * width
    if len(shards) > 0:
        result = level_of(key, dims, shards, -0.22, 0.18) * result
    return jnp.clip(result, min=-most, max=most).astype(kind)


def setup_inputs(seed: int = 0) -> dict:
    arg_keys = jax.random.split(jax.random.key(seed), 14)
    embed_table = noise(arg_keys[0], (F, ROWS, E), 0.7, 5.0, ((0, 4), (1, 64)), jnp.float32)
    accum = jnp.clip(jnp.exp(math.log(3.0) - 3.4011974 * jax.random.uniform(arg_keys[1], (F, ROWS), jnp.float32) ** level_of(arg_keys[1], (F, ROWS), ((0, 4), (1, 64)), -0.2, 0.2)), 0.1, 3.0)
    stale_grad = noise(arg_keys[2], (F, GR, E), 1.0, 6.0, ((0, 4), (1, 64)))
    grad_owner_keys = jax.random.split(jax.random.fold_in(arg_keys[3], 1), F * GR // GR_DEV)
    grad_owner_turns = jax.random.permutation(jax.random.fold_in(arg_keys[3], 3), F * GR // GR_DEV)
    grad_owner = jax.vmap(lambda own, number: deal_out(jax.random.fold_in(arg_keys[3], 2), own, number, GR_DEV, N_DP, 1, GCAP, 2))(grad_owner_keys, grad_owner_turns).reshape((F, GR, 1))
    grad_row = plant(ranked(arg_keys[4], (F, GR), ROWS_DEV, 2), jax.random.fold_in(arg_keys[4], 3), 0, ROWS_DEV - 1).astype(jnp.int32)
    lookup_owner_keys = jax.random.split(jax.random.fold_in(arg_keys[5], 1), F * LOOK // (B_DEV * BAG))
    lookup_owner_turns = jax.random.permutation(jax.random.fold_in(arg_keys[5], 3), F * LOOK // (B_DEV * BAG))
    lookup_owner = jax.vmap(lambda own, number: deal_out(jax.random.fold_in(arg_keys[5], 2), own, number, B_DEV * BAG, N_DP, 1, LCAP, 1))(lookup_owner_keys, lookup_owner_turns).reshape((F, LOOK, 1))
    lookup_row = plant(ranked(arg_keys[6], (F, LOOK), ROWS_DEV, 2), jax.random.fold_in(arg_keys[6], 3), 0, ROWS_DEV - 1).astype(jnp.int32)
    bag_len = plant(jax.random.randint(arg_keys[7], (F, BATCH), 1, BAG + 1), jax.random.fold_in(arg_keys[7], 1), 1, BAG).astype(jnp.int32)
    label = plant((jax.random.randint(arg_keys[8], (BATCH,), 0, 4) < 1).astype(jnp.int32), jax.random.fold_in(arg_keys[8], 1), 0, 1)
    up_factor_weight = noise(arg_keys[9], (LC, R, D0), R ** -0.5, 0.25, ((2, 4),))
    v_weight = noise(arg_keys[10], (LC, R, D0), D0 ** -0.5, 0.09375, ((2, 4),))
    cross_bias = noise(arg_keys[11], (LC, D0), 0.5, 3.0, ((1, 4),), jnp.float32)
    head_weight = noise(arg_keys[12], (D0,), D0 ** -0.5, 0.09375, ((0, 4),), jnp.float32)
    return dict(embed_table=embed_table, accum=accum, stale_grad=stale_grad, grad_owner=grad_owner, grad_row=grad_row, lookup_owner=lookup_owner, lookup_row=lookup_row, bag_len=bag_len, label=label, up_factor_weight=up_factor_weight, v_weight=v_weight, cross_bias=cross_bias, head_weight=head_weight)


learn_rate = 0.5

def adagrad_per_feature(packed):
    table_part, accum_part, grads, target = packed
    summed = jnp.zeros((ROWS, E), jnp.float32).at[target].add(grads.astype(jnp.float32))
    fresh_accum = accum_part + lax.optimization_barrier(jnp.mean(summed * summed, axis=1))
    fresh_table = table_part - learn_rate * summed / jnp.sqrt(fresh_accum)[:, None]
    return (fresh_table, fresh_accum)

def pool_feature(packed):
    table_part, target, counts = packed
    fetched = table_part[target].astype(jnp.bfloat16)
    fetched = lax.optimization_barrier(fetched).astype(jnp.float32).reshape(BATCH, BAG, E)
    inside = (jnp.arange(BAG)[None, :] < counts[:, None]).astype(jnp.float32)
    return lax.optimization_barrier(jnp.sum(fetched * inside[:, :, None], axis=1)).astype(jnp.bfloat16)

def reference(embed_table, accum, stale_grad, grad_owner, grad_row, lookup_owner, lookup_row, bag_len, label, up_factor_weight, v_weight, cross_bias, head_weight):
    grad_target = (grad_owner[:, :, 0] * ROWS_DEV + grad_row).astype(jnp.int32)
    new_table, new_accum = lax.map(adagrad_per_feature, (embed_table, accum, stale_grad, grad_target))
    look_target = (lookup_owner[:, :, 0] * ROWS_DEV + lookup_row).astype(jnp.int32)
    pooled = lax.map(pool_feature, (embed_table, look_target, bag_len))
    start = jnp.transpose(pooled, (1, 0, 2)).reshape(BATCH, D0)
    start_f = start.astype(jnp.float32)
    state = start
    states = []
    downs = []
    crosses = []
    for layer in range(LC):
        down_sum = jnp.dot(state, v_weight[layer].T, preferred_element_type=jnp.float32).astype(jnp.bfloat16)
        cross_out = jnp.dot(down_sum, up_factor_weight[layer], preferred_element_type=jnp.float32) + cross_bias[layer]
        states.append(state)
        downs.append(down_sum)
        crosses.append(cross_out)
        state = (start_f * cross_out + state.astype(jnp.float32)).astype(jnp.bfloat16)
    logit = lax.optimization_barrier(jnp.sum(state.astype(jnp.float32) * head_weight[None, :], axis=1))
    slope = (jax.nn.sigmoid(logit) - label.astype(jnp.float32)) / jnp.sqrt(jnp.float32(BATCH))
    upstream = slope[:, None] * head_weight[None, :]
    head_grad = lax.optimization_barrier(jnp.sum(slope[:, None] * state.astype(jnp.float32), axis=0))
    to_start = jnp.zeros((BATCH, D0), jnp.float32)
    grads_u = [None] * LC
    grads_v = [None] * LC
    bias_grads = [None] * LC
    for layer in reversed(range(LC)):
        direct = upstream * start_f
        bias_grads[layer] = lax.optimization_barrier(jnp.sum(direct, axis=0))
        direct_bias_term = direct.astype(jnp.bfloat16)
        grads_u[layer] = jnp.dot(downs[layer].T, direct_bias_term, preferred_element_type=jnp.float32)
        back_sum = jnp.dot(direct_bias_term, up_factor_weight[layer].T, preferred_element_type=jnp.float32).astype(jnp.bfloat16)
        grads_v[layer] = jnp.dot(back_sum.T, states[layer], preferred_element_type=jnp.float32)
        to_start = to_start + upstream * crosses[layer]
        upstream = upstream + jnp.dot(back_sum, v_weight[layer], preferred_element_type=jnp.float32)
    grad_pooled = (upstream + to_start).astype(jnp.bfloat16)
    grad_small = jnp.stack(bias_grads + [head_grad])
    return (new_table, new_accum, jnp.stack(grads_u), jnp.stack(grads_v), grad_small, grad_pooled)
```

```python
import jax
import jax.numpy as jnp
from jax import lax
from jax.sharding import PartitionSpec as P

learn_rate = 0.5


def in_blocks(array, dim, devices):
    shape = array.shape
    parts = array.reshape(*shape[:dim], devices, shape[dim] // devices, *shape[dim + 1 :])
    return jnp.moveaxis(parts, dim, 0)


def sum_at_owner(array, axis, dim):
    parts = in_blocks(array, dim, lax.axis_size(axis))
    arrived = lax.all_to_all(parts, axis, split_axis=0, concat_axis=0, tiled=True)
    return arrived.sum(axis=0)


def copy_for_each(array, axis):
    copies = jnp.broadcast_to(array, (lax.axis_size(axis), *array.shape))
    return lax.all_to_all(copies, axis, split_axis=0, concat_axis=0, tiled=True)


def over_copies(array, axis):
    return copy_for_each(array, axis).sum(axis=0)


def side_by_side(arrays, axis, dim, along):
    widths = [a.shape[along] for a in arrays]
    both = jnp.concatenate(arrays, axis=along)
    filled = lax.psum_scatter(both, axis, scatter_dimension=dim, tiled=True)
    return tuple(jnp.split(filled, [sum(widths[:k]) for k in range(1, len(widths))], axis=along))


def bucket_slots(owners, capacity, peers):
    count = owners.shape[1]
    onehot = (owners[:, None, :] == jnp.arange(peers)[None, :, None]).astype(jnp.bfloat16)
    earlier = (jnp.arange(count)[:, None] < jnp.arange(count)[None, :]).astype(jnp.bfloat16)
    before = jnp.einsum("fpi,ij->fpj", onehot, earlier, preferred_element_type=jnp.float32)
    order_in = jnp.sum(before * onehot.astype(jnp.float32), axis=1)
    return owners * capacity + order_in.astype(jnp.int32)


def selection_matrix(indices, length):
    return (indices[:, :, None] == jnp.arange(length)[None, None, :]).astype(jnp.bfloat16)


def contract_last(left, right):
    return lax.dot_general(
        left, right, (((1,), (1,)), ((), ())), preferred_element_type=jnp.float32
    )


def contract_first(left, right):
    return lax.dot_general(
        left, right, (((0,), (0,)), ((), ())), preferred_element_type=jnp.float32
    )


def summed_rounded(partial, axis):
    share = lax.psum_scatter(partial, axis, scatter_dimension=0, tiled=True)
    return lax.all_gather(share.astype(jnp.bfloat16), axis, axis=0, tiled=True)


def cross_down(state, v_layer):
    return summed_rounded(contract_last(state, v_layer), "mp")


def local(
    embed_table,
    accum,
    stale_grad,
    grad_owner,
    grad_row,
    lookup_owner,
    lookup_row,
    bag_len,
    label,
    up_factor_weight,
    v_weight,
    cross_bias,
    head_weight,
):
    peers = lax.axis_size("dp")
    local_feats, grad_dev, width = stale_grad.shape
    rows_per_shard = embed_table.shape[1]
    which_feature = jnp.arange(local_feats)[:, None]
    grad_cap = max(2, 2 * grad_dev // peers)
    grad_total = peers * grad_cap
    grad_slot = bucket_slots(grad_owner[:, :, 0], grad_cap, peers)
    place = selection_matrix(grad_slot, grad_total)
    send_grads = jnp.einsum(
        "fns,fne->fse", place, stale_grad, preferred_element_type=jnp.float32
    ).astype(jnp.bfloat16)
    send_rows = (
        jnp.full((local_feats, grad_total), rows_per_shard, jnp.int32)
        .at[which_feature, grad_slot]
        .set(grad_row)
    )
    recv_grads = lax.all_to_all(
        send_grads.reshape(local_feats, peers, grad_cap, width),
        "dp",
        split_axis=1,
        concat_axis=1,
        tiled=True,
    )
    recv_rows = lax.all_to_all(
        send_rows.reshape(local_feats, peers, grad_cap),
        "dp",
        split_axis=1,
        concat_axis=1,
        tiled=True,
    )
    landing = selection_matrix(recv_rows.reshape(local_feats, grad_total), rows_per_shard)
    summed = jnp.einsum(
        "wjc,wjl->wcl",
        landing,
        recv_grads.reshape(local_feats, grad_total, width),
        preferred_element_type=jnp.float32,
    )
    new_accum = accum + jnp.mean(summed * summed, axis=2)
    new_table = embed_table - learn_rate * summed / jnp.sqrt(new_accum)[:, :, None]
    batch_dev = bag_len.shape[1]
    look_dev = lookup_row.shape[1]
    bag_size = look_dev // batch_dev
    look_cap = max(2, 2 * look_dev // peers)
    look_total = peers * look_cap
    look_slot = bucket_slots(lookup_owner[:, :, 0], look_cap, peers)
    wanted = (
        jnp.zeros((local_feats, look_total), jnp.int32).at[which_feature, look_slot].set(lookup_row)
    )
    requested_ids = lax.all_to_all(
        wanted.reshape(local_feats, peers, look_cap), "dp", split_axis=1, concat_axis=1, tiled=True
    ).reshape(local_feats, look_total)
    second_table = embed_table.astype(jnp.bfloat16)
    served = jnp.einsum(
        "adv,avm->adm",
        selection_matrix(requested_ids, rows_per_shard),
        second_table,
        preferred_element_type=jnp.float32,
    ).astype(jnp.bfloat16)
    returned = lax.all_to_all(
        served.reshape(local_feats, peers, look_cap, width),
        "dp",
        split_axis=1,
        concat_axis=1,
        tiled=True,
    ).reshape(local_feats, look_total, width)
    slots = look_slot.reshape(local_feats, batch_dev, bag_size)
    mixing = jnp.zeros((local_feats, batch_dev, look_total), jnp.bfloat16)
    for member in range(bag_size):
        used = (bag_len > member).astype(jnp.bfloat16)
        mixing = mixing + selection_matrix(slots[:, :, member], look_total) * used[:, :, None]
    pooled = jnp.einsum(
        "fbs,fse->fbe", mixing, returned, preferred_element_type=jnp.float32
    ).astype(jnp.bfloat16)
    start = jnp.transpose(pooled, (1, 0, 2)).reshape(batch_dev, local_feats * width)
    start_f = start.astype(jnp.float32)
    n_layers = up_factor_weight.shape[0]
    state = start
    states = []
    downs = []
    crosses = []
    for layer in range(n_layers):
        down_sum = cross_down(state, v_weight[layer])
        cross_out = (
            jnp.dot(down_sum, up_factor_weight[layer], preferred_element_type=jnp.float32)
            + cross_bias[layer]
        )
        states.append(state)
        downs.append(down_sum)
        crosses.append(cross_out)
        state = (start_f * cross_out + state.astype(jnp.float32)).astype(jnp.bfloat16)
    logit = lax.psum(jnp.sum(state.astype(jnp.float32) * head_weight[None, :], axis=1), "mp")
    slope = (jax.nn.sigmoid(logit) - label.astype(jnp.float32)) / jnp.sqrt(
        jnp.float32(batch_dev * peers)
    )
    upstream = slope[:, None] * head_weight[None, :]
    head_grad = jnp.sum(slope[:, None] * state.astype(jnp.float32), axis=0)
    to_start = jnp.zeros(start_f.shape, jnp.float32)
    grads_u = [None] * n_layers
    grads_v = [None] * n_layers
    bias_grads = [None] * n_layers
    for layer in reversed(range(n_layers)):
        direct = upstream * start_f
        bias_grads[layer] = jnp.sum(direct, axis=0)
        direct_bias_term = direct.astype(jnp.bfloat16)
        grad_u_layer = contract_first(downs[layer], direct_bias_term)
        back_sum = summed_rounded(
            contract_last(direct_bias_term, up_factor_weight[layer]), "mp"
        )
        down_factor_gradient = contract_first(back_sum, states[layer])
        to_start = to_start + upstream * crosses[layer]
        upstream = upstream + jnp.dot(back_sum, v_weight[layer], preferred_element_type=jnp.float32)
        grads_u[layer] = grad_u_layer
        grads_v[layer] = down_factor_gradient
    grad_u = jnp.stack(grads_u)
    grad_v = jnp.stack(grads_v)
    grad_u, grad_v = side_by_side((grad_u, grad_v), "dp", 1, 0)
    grad_small = lax.psum(jnp.stack(bias_grads + [head_grad]), "dp")
    grad_pooled = (upstream + to_start).astype(jnp.bfloat16)
    return (new_table, new_accum, grad_u, grad_v, grad_small, grad_pooled)


def solution(mesh):
    return jax.shard_map(
        local,
        mesh=mesh,
        in_specs=(
            P("mp", "dp", None),
            P("mp", "dp"),
            P("mp", "dp", None),
            P("mp", "dp", None),
            P("mp", "dp"),
            P("mp", "dp", None),
            P("mp", "dp"),
            P("mp", "dp"),
            P("dp"),
            P(None, None, "mp"),
            P(None, None, "mp"),
            P(None, "mp"),
            P("mp"),
        ),
        out_specs=(
            P("mp", "dp", None),
            P("mp", "dp"),
            P(None, "dp", "mp"),
            P(None, "dp", "mp"),
            P(None, "mp"),
            P("dp", "mp"),
        ),
        check_vma=False,
    )
```

```python
import jax
import jax.numpy as jnp
from jax import lax
from jax.sharding import PartitionSpec as P

learn_rate = 0.5


def in_blocks(array, dim, devices):
    shape = array.shape
    parts = array.reshape(*shape[:dim], devices, shape[dim] // devices, *shape[dim + 1 :])
    return jnp.moveaxis(parts, dim, 0)


def sum_at_owner(array, axis, dim):
    parts = in_blocks(array, dim, lax.axis_size(axis))
    arrived = lax.all_to_all(parts, axis, split_axis=0, concat_axis=0, tiled=True)
    return arrived.sum(axis=0)


def copy_for_each(array, axis):
    copies = jnp.broadcast_to(array, (lax.axis_size(axis), *array.shape))
    return lax.all_to_all(copies, axis, split_axis=0, concat_axis=0, tiled=True)


def over_copies(array, axis):
    return copy_for_each(array, axis).sum(axis=0)


def side_by_side(arrays, axis, dim, along):
    widths = [a.shape[along] for a in arrays]
    both = jnp.concatenate(arrays, axis=along)
    filled = lax.psum_scatter(both, axis, scatter_dimension=dim, tiled=True)
    return tuple(jnp.split(filled, [sum(widths[:k]) for k in range(1, len(widths))], axis=along))


def bucket_slots(owners, capacity, peers):
    count = owners.shape[1]
    onehot = (owners[:, None, :] == jnp.arange(peers)[None, :, None]).astype(jnp.bfloat16)
    earlier = (jnp.arange(count)[:, None] < jnp.arange(count)[None, :]).astype(jnp.bfloat16)
    before = jnp.einsum("fpi,ij->fpj", onehot, earlier, preferred_element_type=jnp.float32)
    order_in = jnp.sum(before * onehot.astype(jnp.float32), axis=1)
    return owners * capacity + order_in.astype(jnp.int32)


def selection_matrix(indices, length):
    return (indices[:, :, None] == jnp.arange(length)[None, None, :]).astype(jnp.bfloat16)


def contract_last(left, right):
    return lax.dot_general(
        left, right, (((1,), (1,)), ((), ())), preferred_element_type=jnp.float32
    )


def contract_first(left, right):
    return lax.dot_general(
        left, right, (((0,), (0,)), ((), ())), preferred_element_type=jnp.float32
    )


def summed_rounded(partial, axis):
    return lax.all_gather(partial, axis, axis=0).sum(axis=0).astype(jnp.bfloat16)


def cross_down(state, v_layer):
    return summed_rounded(contract_last(state, v_layer), "mp")


def local(
    embed_table,
    accum,
    stale_grad,
    grad_owner,
    grad_row,
    lookup_owner,
    lookup_row,
    bag_len,
    label,
    up_factor_weight,
    v_weight,
    cross_bias,
    head_weight,
):
    peers = lax.axis_size("dp")
    local_feats, grad_dev, width = stale_grad.shape
    rows_per_shard = embed_table.shape[1]
    which_feature = jnp.arange(local_feats)[:, None]
    grad_cap = max(2, 2 * grad_dev // peers)
    grad_total = peers * grad_cap
    grad_slot = bucket_slots(grad_owner[:, :, 0], grad_cap, peers)
    place = selection_matrix(grad_slot, grad_total)
    send_grads = jnp.einsum(
        "fns,fne->fse", place, stale_grad, preferred_element_type=jnp.float32
    ).astype(jnp.bfloat16)
    send_rows = (
        jnp.full((local_feats, grad_total), rows_per_shard, jnp.int32)
        .at[which_feature, grad_slot]
        .set(grad_row)
    )
    batch_dev = bag_len.shape[1]
    look_dev = lookup_row.shape[1]
    bag_size = look_dev // batch_dev
    look_cap = max(2, 2 * look_dev // peers)
    look_total = peers * look_cap
    look_slot = bucket_slots(lookup_owner[:, :, 0], look_cap, peers)
    wanted = (
        jnp.zeros((local_feats, look_total), jnp.int32).at[which_feature, look_slot].set(lookup_row)
    )
    requested_ids = lax.all_to_all(
        wanted.reshape(local_feats, peers, look_cap), "dp", split_axis=1, concat_axis=1, tiled=True
    ).reshape(local_feats, look_total)
    second_table = embed_table.astype(jnp.bfloat16)
    served = jnp.einsum(
        "adv,avm->adm",
        selection_matrix(requested_ids, rows_per_shard),
        second_table,
        preferred_element_type=jnp.float32,
    ).astype(jnp.bfloat16)
    returned = lax.all_to_all(
        served.reshape(local_feats, peers, look_cap, width),
        "dp",
        split_axis=1,
        concat_axis=1,
        tiled=True,
    ).reshape(local_feats, look_total, width)
    slots = look_slot.reshape(local_feats, batch_dev, bag_size)
    mixing = jnp.zeros((local_feats, batch_dev, look_total), jnp.bfloat16)
    for member in range(bag_size):
        used = (bag_len > member).astype(jnp.bfloat16)
        mixing = mixing + selection_matrix(slots[:, :, member], look_total) * used[:, :, None]
    pooled = jnp.einsum(
        "fbs,fse->fbe", mixing, returned, preferred_element_type=jnp.float32
    ).astype(jnp.bfloat16)
    start = jnp.transpose(pooled, (1, 0, 2)).reshape(batch_dev, local_feats * width)
    send_grads, send_rows, start = lax.optimization_barrier((send_grads, send_rows, start))
    recv_grads = lax.all_to_all(
        send_grads.reshape(local_feats, peers, grad_cap, width),
        "dp",
        split_axis=1,
        concat_axis=1,
        tiled=True,
    )
    recv_rows = lax.all_to_all(
        send_rows.reshape(local_feats, peers, grad_cap),
        "dp",
        split_axis=1,
        concat_axis=1,
        tiled=True,
    )
    start_f = start.astype(jnp.float32)
    n_layers = up_factor_weight.shape[0]
    state = start
    states = []
    downs = []
    crosses = []
    for layer in range(n_layers):
        down_sum = cross_down(state, v_weight[layer])
        cross_out = (
            jnp.dot(down_sum, up_factor_weight[layer], preferred_element_type=jnp.float32)
            + cross_bias[layer]
        )
        states.append(state)
        downs.append(down_sum)
        crosses.append(cross_out)
        state = (start_f * cross_out + state.astype(jnp.float32)).astype(jnp.bfloat16)
    local_logit = jnp.sum(state.astype(jnp.float32) * head_weight[None, :], axis=1)
    recv_grads, recv_rows, local_logit = lax.optimization_barrier(
        (recv_grads, recv_rows, local_logit)
    )
    logit = lax.psum(local_logit, "mp")
    slope = (jax.nn.sigmoid(logit) - label.astype(jnp.float32)) / jnp.sqrt(
        jnp.float32(batch_dev * peers)
    )
    upstream = slope[:, None] * head_weight[None, :]
    head_grad = jnp.sum(slope[:, None] * state.astype(jnp.float32), axis=0)
    to_start = jnp.zeros(start_f.shape, jnp.float32)
    grads_u = [None] * n_layers
    grads_v = [None] * n_layers
    bias_grads = [None] * n_layers
    for layer in reversed(range(n_layers)):
        direct = upstream * start_f
        bias_grads[layer] = jnp.sum(direct, axis=0)
        direct_bias_term = direct.astype(jnp.bfloat16)
        grad_u_layer = contract_first(downs[layer], direct_bias_term)
        back_sum = summed_rounded(
            contract_last(direct_bias_term, up_factor_weight[layer]), "mp"
        )
        down_factor_gradient = contract_first(back_sum, states[layer])
        to_start = to_start + upstream * crosses[layer]
        upstream = upstream + jnp.dot(back_sum, v_weight[layer], preferred_element_type=jnp.float32)
        grads_u[layer] = grad_u_layer
        grads_v[layer] = down_factor_gradient
    landing = selection_matrix(recv_rows.reshape(local_feats, grad_total), rows_per_shard)
    summed = jnp.einsum(
        "wjc,wjl->wcl",
        landing,
        recv_grads.reshape(local_feats, grad_total, width),
        preferred_element_type=jnp.float32,
    )
    new_accum = accum + jnp.mean(summed * summed, axis=2)
    new_table = embed_table - learn_rate * summed / jnp.sqrt(new_accum)[:, :, None]
    grad_u = jnp.stack(grads_u)
    grad_v = jnp.stack(grads_v)
    small = jnp.stack(bias_grads + [head_grad])
    both = jnp.concatenate((grad_u, grad_v), axis=0)
    lead, rows, cols = both.shape
    block_rows = rows // peers
    extra = -(-small.size // (lead * block_rows * 128)) * 128
    small_block = jnp.pad(small.reshape(-1), (0, lead * block_rows * extra - small.size))
    small_rep = jnp.tile(small_block.reshape(lead, block_rows, extra), (1, peers, 1))
    filled = lax.psum_scatter(
        jnp.concatenate((both, small_rep), axis=2), "dp", scatter_dimension=1, tiled=True
    )
    grad_u, grad_v = jnp.split(filled[:, :, :cols], 2, axis=0)
    grad_small = filled[:, :, cols:].reshape(-1)[: small.size].reshape(small.shape)
    grad_pooled = (upstream + to_start).astype(jnp.bfloat16)
    return (new_table, new_accum, grad_u, grad_v, grad_small, grad_pooled)


def solution(mesh):
    return jax.shard_map(
        local,
        mesh=mesh,
        in_specs=(
            P("mp", "dp", None),
            P("mp", "dp"),
            P("mp", "dp", None),
            P("mp", "dp", None),
            P("mp", "dp"),
            P("mp", "dp", None),
            P("mp", "dp"),
            P("mp", "dp"),
            P("dp"),
            P(None, None, "mp"),
            P(None, None, "mp"),
            P(None, "mp"),
            P("mp"),
        ),
        out_specs=(
            P("mp", "dp", None),
            P("mp", "dp"),
            P(None, "dp", "mp"),
            P(None, "dp", "mp"),
            P(None, "mp"),
            P("dp", "mp"),
        ),
        check_vma=False,
    )
```

```python
import jax
import jax.numpy as jnp
from jax import lax
from jax.sharding import PartitionSpec as P

learn_rate = 0.5


def in_blocks(array, dim, devices):
    shape = array.shape
    parts = array.reshape(*shape[:dim], devices, shape[dim] // devices, *shape[dim + 1 :])
    return jnp.moveaxis(parts, dim, 0)


def sum_at_owner(array, axis, dim):
    parts = in_blocks(array, dim, lax.axis_size(axis))
    arrived = lax.all_to_all(parts, axis, split_axis=0, concat_axis=0, tiled=True)
    return arrived.sum(axis=0)


def copy_for_each(array, axis):
    copies = jnp.broadcast_to(array, (lax.axis_size(axis), *array.shape))
    return lax.all_to_all(copies, axis, split_axis=0, concat_axis=0, tiled=True)


def over_copies(array, axis):
    return copy_for_each(array, axis).sum(axis=0)


def side_by_side(arrays, axis, dim, along):
    widths = [a.shape[along] for a in arrays]
    both = jnp.concatenate(arrays, axis=along)
    filled = lax.psum_scatter(both, axis, scatter_dimension=dim, tiled=True)
    return tuple(jnp.split(filled, [sum(widths[:k]) for k in range(1, len(widths))], axis=along))


def bucket_slots(owners, capacity, peers):
    count = owners.shape[1]
    onehot = (owners[:, None, :] == jnp.arange(peers)[None, :, None]).astype(jnp.bfloat16)
    earlier = (jnp.arange(count)[:, None] < jnp.arange(count)[None, :]).astype(jnp.bfloat16)
    before = jnp.einsum("fpi,ij->fpj", onehot, earlier, preferred_element_type=jnp.float32)
    order_in = jnp.sum(before * onehot.astype(jnp.float32), axis=1)
    return owners * capacity + order_in.astype(jnp.int32)


def selection_matrix(indices, length):
    return (indices[:, :, None] == jnp.arange(length)[None, None, :]).astype(jnp.bfloat16)


def contract_last(left, right):
    return lax.dot_general(
        left, right, (((1,), (1,)), ((), ())), preferred_element_type=jnp.float32
    )


def contract_first(left, right):
    return lax.dot_general(
        left, right, (((0,), (0,)), ((), ())), preferred_element_type=jnp.float32
    )


def cross_down(state, v_layer):
    share = sum_at_owner(contract_last(state, v_layer), "mp", 0)
    return lax.all_gather(share.astype(jnp.bfloat16), "mp", axis=0, tiled=True)


def local(
    embed_table,
    accum,
    stale_grad,
    grad_owner,
    grad_row,
    lookup_owner,
    lookup_row,
    bag_len,
    label,
    up_factor_weight,
    v_weight,
    cross_bias,
    head_weight,
):
    peers = lax.axis_size("dp")
    local_feats, grad_dev, width = stale_grad.shape
    rows_per_shard = embed_table.shape[1]
    which_feature = jnp.arange(local_feats)[:, None]
    grad_cap = max(2, 2 * grad_dev // peers)
    grad_total = peers * grad_cap
    grad_slot = bucket_slots(grad_owner[:, :, 0], grad_cap, peers)
    place = selection_matrix(grad_slot, grad_total)
    send_grads = jnp.einsum(
        "fns,fne->fse", place, stale_grad, preferred_element_type=jnp.float32
    ).astype(jnp.bfloat16)
    send_rows = (
        jnp.full((local_feats, grad_total), rows_per_shard, jnp.int32)
        .at[which_feature, grad_slot]
        .set(grad_row)
    )
    recv_grads = lax.all_to_all(
        send_grads.reshape(local_feats, peers, grad_cap, width),
        "dp",
        split_axis=1,
        concat_axis=1,
        tiled=True,
    )
    batch_dev = bag_len.shape[1]
    look_dev = lookup_row.shape[1]
    bag_size = look_dev // batch_dev
    look_cap = max(2, 2 * look_dev // peers)
    look_total = peers * look_cap
    look_slot = bucket_slots(lookup_owner[:, :, 0], look_cap, peers)
    wanted = (
        jnp.zeros((local_feats, look_total), jnp.int32).at[which_feature, look_slot].set(lookup_row)
    )
    both_ids = jnp.concatenate(
        (wanted.reshape(local_feats, peers, look_cap), send_rows.reshape(local_feats, peers, grad_cap)),
        axis=2,
    )
    both_ids = lax.all_to_all(both_ids, "dp", split_axis=1, concat_axis=1, tiled=True)
    requested_ids = both_ids[:, :, :look_cap].reshape(local_feats, look_total)
    recv_rows = both_ids[:, :, look_cap:]
    landing = selection_matrix(recv_rows.reshape(local_feats, grad_total), rows_per_shard)
    summed = jnp.einsum(
        "wjc,wjl->wcl",
        landing,
        recv_grads.reshape(local_feats, grad_total, width),
        preferred_element_type=jnp.float32,
    )
    new_accum = accum + jnp.mean(summed * summed, axis=2)
    new_table = embed_table - learn_rate * summed / jnp.sqrt(new_accum)[:, :, None]
    second_table = embed_table.astype(jnp.bfloat16)
    served = jnp.einsum(
        "adv,avm->adm",
        selection_matrix(requested_ids, rows_per_shard),
        second_table,
        preferred_element_type=jnp.float32,
    ).astype(jnp.bfloat16)
    returned = lax.all_to_all(
        served.reshape(local_feats, peers, look_cap, width),
        "dp",
        split_axis=1,
        concat_axis=1,
        tiled=True,
    ).reshape(local_feats, look_total, width)
    slots = look_slot.reshape(local_feats, batch_dev, bag_size)
    mixing = jnp.zeros((local_feats, batch_dev, look_total), jnp.bfloat16)
    for member in range(bag_size):
        used = (bag_len > member).astype(jnp.bfloat16)
        mixing = mixing + selection_matrix(slots[:, :, member], look_total) * used[:, :, None]
    pooled = jnp.einsum(
        "fbs,fse->fbe", mixing, returned, preferred_element_type=jnp.float32
    ).astype(jnp.bfloat16)
    start = jnp.transpose(pooled, (1, 0, 2)).reshape(batch_dev, local_feats * width)
    start_f = start.astype(jnp.float32)
    n_layers = up_factor_weight.shape[0]
    state = start
    states = []
    downs = []
    crosses = []
    for layer in range(n_layers):
        down_sum = cross_down(state, v_weight[layer])
        cross_out = (
            jnp.dot(down_sum, up_factor_weight[layer], preferred_element_type=jnp.float32)
            + cross_bias[layer]
        )
        states.append(state)
        downs.append(down_sum)
        crosses.append(cross_out)
        state = (start_f * cross_out + state.astype(jnp.float32)).astype(jnp.bfloat16)
    logit = lax.psum(jnp.sum(state.astype(jnp.float32) * head_weight[None, :], axis=1), "mp")
    slope = (jax.nn.sigmoid(logit) - label.astype(jnp.float32)) / jnp.sqrt(
        jnp.float32(batch_dev * peers)
    )
    upstream = slope[:, None] * head_weight[None, :]
    head_grad = jnp.sum(slope[:, None] * state.astype(jnp.float32), axis=0)
    to_start = jnp.zeros(start_f.shape, jnp.float32)
    grads_u = [None] * n_layers
    grads_v = [None] * n_layers
    bias_grads = [None] * n_layers
    for layer in reversed(range(n_layers)):
        direct = upstream * start_f
        bias_grads[layer] = jnp.sum(direct, axis=0)
        direct_bias_term = direct.astype(jnp.bfloat16)
        grad_u_layer = contract_first(downs[layer], direct_bias_term)
        back_sum = over_copies(
            contract_last(direct_bias_term, up_factor_weight[layer]), "mp"
        ).astype(jnp.bfloat16)
        down_factor_gradient = contract_first(back_sum, states[layer])
        to_start = to_start + upstream * crosses[layer]
        upstream = upstream + jnp.dot(back_sum, v_weight[layer], preferred_element_type=jnp.float32)
        grads_u[layer] = grad_u_layer
        grads_v[layer] = down_factor_gradient
    small = jnp.stack(bias_grads + [head_grad])
    rest = lax.psum_scatter(
        jnp.stack((grads_u[1], grads_v[1], grads_v[0])), "dp", scatter_dimension=1, tiled=True
    )
    parts_u = in_blocks(grads_u[0], 0, peers)
    block_rows, cols = parts_u.shape[1:]
    small_rows = jnp.broadcast_to(small.reshape(block_rows, -1), (peers, block_rows, small.size // block_rows))
    arrived = lax.all_to_all(
        jnp.concatenate((parts_u, small_rows), axis=2), "dp", split_axis=0, concat_axis=0, tiled=True
    ).sum(axis=0)
    grad_u = jnp.stack((arrived[:, :cols], rest[0]))
    grad_v = jnp.stack((rest[2], rest[1]))
    grad_small = arrived[:, cols:].reshape(small.shape)
    grad_pooled = (upstream + to_start).astype(jnp.bfloat16)
    return (new_table, new_accum, grad_u, grad_v, grad_small, grad_pooled)


def solution(mesh):
    return jax.shard_map(
        local,
        mesh=mesh,
        in_specs=(
            P("mp", "dp", None),
            P("mp", "dp"),
            P("mp", "dp", None),
            P("mp", "dp", None),
            P("mp", "dp"),
            P("mp", "dp", None),
            P("mp", "dp"),
            P("mp", "dp"),
            P("dp"),
            P(None, None, "mp"),
            P(None, None, "mp"),
            P(None, "mp"),
            P("mp"),
        ),
        out_specs=(
            P("mp", "dp", None),
            P("mp", "dp"),
            P(None, "dp", "mp"),
            P(None, "dp", "mp"),
            P(None, "mp"),
            P("dp", "mp"),
        ),
        check_vma=False,
    )
```

```python
import jax
import jax.numpy as jnp
from jax import lax
from jax.sharding import PartitionSpec as P

learn_rate = 0.5


def in_blocks(array, dim, devices):
    shape = array.shape
    parts = array.reshape(*shape[:dim], devices, shape[dim] // devices, *shape[dim + 1 :])
    return jnp.moveaxis(parts, dim, 0)


def sum_at_owner(array, axis, dim):
    parts = in_blocks(array, dim, lax.axis_size(axis))
    arrived = lax.all_to_all(parts, axis, split_axis=0, concat_axis=0, tiled=True)
    return arrived.sum(axis=0)


def copy_for_each(array, axis):
    copies = jnp.broadcast_to(array, (lax.axis_size(axis), *array.shape))
    return lax.all_to_all(copies, axis, split_axis=0, concat_axis=0, tiled=True)


def over_copies(array, axis):
    return copy_for_each(array, axis).sum(axis=0)


def butterfly_sum(array, axis):
    peers = lax.axis_size(axis)
    step = 1
    while step < peers:
        array = array + lax.ppermute(array, axis, [(i, i ^ step) for i in range(peers)])
        step *= 2
    return array


def side_by_side(arrays, axis, dim, along):
    widths = [a.shape[along] for a in arrays]
    both = jnp.concatenate(arrays, axis=along)
    filled = lax.psum_scatter(both, axis, scatter_dimension=dim, tiled=True)
    return tuple(jnp.split(filled, [sum(widths[:k]) for k in range(1, len(widths))], axis=along))


def bucket_slots(owners, capacity, peers):
    count = owners.shape[1]
    onehot = (owners[:, None, :] == jnp.arange(peers)[None, :, None]).astype(jnp.bfloat16)
    earlier = (jnp.arange(count)[:, None] < jnp.arange(count)[None, :]).astype(jnp.bfloat16)
    before = jnp.einsum("fpi,ij->fpj", onehot, earlier, preferred_element_type=jnp.float32)
    order_in = jnp.sum(before * onehot.astype(jnp.float32), axis=1)
    return owners * capacity + order_in.astype(jnp.int32)


def selection_matrix(indices, length):
    return (indices[:, :, None] == jnp.arange(length)[None, None, :]).astype(jnp.bfloat16)


def contract_last(left, right):
    return lax.dot_general(
        left, right, (((1,), (1,)), ((), ())), preferred_element_type=jnp.float32
    )


def contract_first(left, right):
    return lax.dot_general(
        left, right, (((0,), (0,)), ((), ())), preferred_element_type=jnp.float32
    )


def cross_down(state, v_layer):
    share = sum_at_owner(contract_last(state, v_layer), "mp", 0)
    return lax.all_gather(share.astype(jnp.bfloat16), "mp", axis=0, tiled=True)


def local(
    embed_table,
    accum,
    stale_grad,
    grad_owner,
    grad_row,
    lookup_owner,
    lookup_row,
    bag_len,
    label,
    up_factor_weight,
    v_weight,
    cross_bias,
    head_weight,
):
    peers = lax.axis_size("dp")
    local_feats, grad_dev, width = stale_grad.shape
    rows_per_shard = embed_table.shape[1]
    which_feature = jnp.arange(local_feats)[:, None]
    grad_cap = max(2, 2 * grad_dev // peers)
    grad_total = peers * grad_cap
    grad_slot = bucket_slots(grad_owner[:, :, 0], grad_cap, peers)
    place = selection_matrix(grad_slot, grad_total)
    send_grads = jnp.einsum(
        "fns,fne->fse", place, stale_grad, preferred_element_type=jnp.float32
    ).astype(jnp.bfloat16)
    send_rows = (
        jnp.full((local_feats, grad_total), rows_per_shard, jnp.int32)
        .at[which_feature, grad_slot]
        .set(grad_row)
    )
    batch_dev = bag_len.shape[1]
    look_dev = lookup_row.shape[1]
    bag_size = look_dev // batch_dev
    look_cap = max(2, 2 * look_dev // peers)
    look_total = peers * look_cap
    look_slot = bucket_slots(lookup_owner[:, :, 0], look_cap, peers)
    wanted = (
        jnp.zeros((local_feats, look_total), jnp.int32).at[which_feature, look_slot].set(lookup_row)
    )
    both_ids = jnp.concatenate(
        (wanted.reshape(local_feats, peers, look_cap), send_rows.reshape(local_feats, peers, grad_cap)),
        axis=2,
    )
    both_ids = lax.all_to_all(both_ids, "dp", split_axis=1, concat_axis=1, tiled=True)
    requested_ids = both_ids[:, :, :look_cap].reshape(local_feats, look_total)
    recv_rows = both_ids[:, :, look_cap:]
    second_table = embed_table.astype(jnp.bfloat16)
    served = jnp.einsum(
        "adv,avm->adm",
        selection_matrix(requested_ids, rows_per_shard),
        second_table,
        preferred_element_type=jnp.float32,
    ).astype(jnp.bfloat16)
    returned = lax.all_to_all(
        served.reshape(local_feats, peers, look_cap, width),
        "dp",
        split_axis=1,
        concat_axis=1,
        tiled=True,
    ).reshape(local_feats, look_total, width)
    slots = look_slot.reshape(local_feats, batch_dev, bag_size)
    mixing = jnp.zeros((local_feats, batch_dev, look_total), jnp.bfloat16)
    for member in range(bag_size):
        used = (bag_len > member).astype(jnp.bfloat16)
        mixing = mixing + selection_matrix(slots[:, :, member], look_total) * used[:, :, None]
    pooled = jnp.einsum(
        "fbs,fse->fbe", mixing, returned, preferred_element_type=jnp.float32
    ).astype(jnp.bfloat16)
    start = jnp.transpose(pooled, (1, 0, 2)).reshape(batch_dev, local_feats * width)
    send_grads, start = lax.optimization_barrier((send_grads, start))
    recv_grads = lax.all_to_all(
        send_grads.reshape(local_feats, peers, grad_cap, width),
        "dp",
        split_axis=1,
        concat_axis=1,
        tiled=True,
    )
    start_f = start.astype(jnp.float32)
    n_layers = up_factor_weight.shape[0]
    state = start
    states = []
    downs = []
    crosses = []
    for layer in range(n_layers):
        down_sum = cross_down(state, v_weight[layer])
        cross_out = (
            jnp.dot(down_sum, up_factor_weight[layer], preferred_element_type=jnp.float32)
            + cross_bias[layer]
        )
        states.append(state)
        downs.append(down_sum)
        crosses.append(cross_out)
        state = (start_f * cross_out + state.astype(jnp.float32)).astype(jnp.bfloat16)
    local_logit = jnp.sum(state.astype(jnp.float32) * head_weight[None, :], axis=1)
    recv_grads, local_logit = lax.optimization_barrier((recv_grads, local_logit))
    logit = lax.psum(local_logit, "mp")
    slope = (jax.nn.sigmoid(logit) - label.astype(jnp.float32)) / jnp.sqrt(
        jnp.float32(batch_dev * peers)
    )
    upstream = slope[:, None] * head_weight[None, :]
    head_grad = jnp.sum(slope[:, None] * state.astype(jnp.float32), axis=0)
    to_start = jnp.zeros(start_f.shape, jnp.float32)
    grads_u = [None] * n_layers
    grads_v = [None] * n_layers
    bias_grads = [None] * n_layers
    for layer in reversed(range(n_layers)):
        direct = upstream * start_f
        bias_grads[layer] = jnp.sum(direct, axis=0)
        direct_bias_term = direct.astype(jnp.bfloat16)
        grad_u_layer = contract_first(downs[layer], direct_bias_term)
        back_sum = over_copies(
            contract_last(direct_bias_term, up_factor_weight[layer]), "mp"
        ).astype(jnp.bfloat16)
        down_factor_gradient = contract_first(back_sum, states[layer])
        to_start = to_start + upstream * crosses[layer]
        upstream = upstream + jnp.dot(back_sum, v_weight[layer], preferred_element_type=jnp.float32)
        grads_u[layer] = grad_u_layer
        grads_v[layer] = down_factor_gradient
    landing = selection_matrix(recv_rows.reshape(local_feats, grad_total), rows_per_shard)
    summed = jnp.einsum(
        "wjc,wjl->wcl",
        landing,
        recv_grads.reshape(local_feats, grad_total, width),
        preferred_element_type=jnp.float32,
    )
    new_accum = accum + jnp.mean(summed * summed, axis=2)
    new_table = embed_table - learn_rate * summed / jnp.sqrt(new_accum)[:, :, None]
    grad_u = jnp.stack(grads_u)
    grad_v = jnp.stack(grads_v)
    grad_u, grad_v = side_by_side((grad_u, grad_v), "dp", 1, 0)
    grad_small = butterfly_sum(jnp.stack(bias_grads + [head_grad]), "dp")
    grad_pooled = (upstream + to_start).astype(jnp.bfloat16)
    return (new_table, new_accum, grad_u, grad_v, grad_small, grad_pooled)


def solution(mesh):
    return jax.shard_map(
        local,
        mesh=mesh,
        in_specs=(
            P("mp", "dp", None),
            P("mp", "dp"),
            P("mp", "dp", None),
            P("mp", "dp", None),
            P("mp", "dp"),
            P("mp", "dp", None),
            P("mp", "dp"),
            P("mp", "dp"),
            P("dp"),
            P(None, None, "mp"),
            P(None, None, "mp"),
            P(None, "mp"),
            P("mp"),
        ),
        out_specs=(
            P("mp", "dp", None),
            P("mp", "dp"),
            P(None, "dp", "mp"),
            P(None, "dp", "mp"),
            P(None, "mp"),
            P("dp", "mp"),
        ),
        check_vma=False,
    )
```

```python
import jax
import jax.numpy as jnp
from jax import lax
from jax.sharding import PartitionSpec as P

learn_rate = 0.5


def in_blocks(array, dim, devices):
    shape = array.shape
    parts = array.reshape(*shape[:dim], devices, shape[dim] // devices, *shape[dim + 1 :])
    return jnp.moveaxis(parts, dim, 0)


def sum_at_owner(array, axis, dim):
    parts = in_blocks(array, dim, lax.axis_size(axis))
    arrived = lax.all_to_all(parts, axis, split_axis=0, concat_axis=0, tiled=True)
    return arrived.sum(axis=0)


def copy_for_each(array, axis):
    copies = jnp.broadcast_to(array, (lax.axis_size(axis), *array.shape))
    return lax.all_to_all(copies, axis, split_axis=0, concat_axis=0, tiled=True)


def over_copies(array, axis):
    return copy_for_each(array, axis).sum(axis=0)


def butterfly_sum(array, axis):
    peers = lax.axis_size(axis)
    step = 1
    while step < peers:
        array = array + lax.ppermute(array, axis, [(i, i ^ step) for i in range(peers)])
        step *= 2
    return array


def side_by_side(arrays, axis, dim, along):
    widths = [a.shape[along] for a in arrays]
    both = jnp.concatenate(arrays, axis=along)
    filled = lax.psum_scatter(both, axis, scatter_dimension=dim, tiled=True)
    return tuple(jnp.split(filled, [sum(widths[:k]) for k in range(1, len(widths))], axis=along))


def bucket_slots(owners, capacity, peers):
    count = owners.shape[1]
    onehot = (owners[:, None, :] == jnp.arange(peers)[None, :, None]).astype(jnp.bfloat16)
    earlier = (jnp.arange(count)[:, None] < jnp.arange(count)[None, :]).astype(jnp.bfloat16)
    before = jnp.einsum("fpi,ij->fpj", onehot, earlier, preferred_element_type=jnp.float32)
    order_in = jnp.sum(before * onehot.astype(jnp.float32), axis=1)
    return owners * capacity + order_in.astype(jnp.int32)


def selection_matrix(indices, length):
    return (indices[:, :, None] == jnp.arange(length)[None, None, :]).astype(jnp.bfloat16)


def contract_last(left, right):
    return lax.dot_general(
        left, right, (((1,), (1,)), ((), ())), preferred_element_type=jnp.float32
    )


def contract_first(left, right):
    return lax.dot_general(
        left, right, (((0,), (0,)), ((), ())), preferred_element_type=jnp.float32
    )


def cross_down(state, v_layer):
    return over_copies(contract_last(state, v_layer), "mp").astype(jnp.bfloat16)


def local(
    embed_table,
    accum,
    stale_grad,
    grad_owner,
    grad_row,
    lookup_owner,
    lookup_row,
    bag_len,
    label,
    up_factor_weight,
    v_weight,
    cross_bias,
    head_weight,
):
    peers = lax.axis_size("dp")
    local_feats, grad_dev, width = stale_grad.shape
    rows_per_shard = embed_table.shape[1]
    which_feature = jnp.arange(local_feats)[:, None]
    grad_cap = max(2, 2 * grad_dev // peers)
    grad_total = peers * grad_cap
    grad_slot = bucket_slots(grad_owner[:, :, 0], grad_cap, peers)
    place = selection_matrix(grad_slot, grad_total)
    send_grads = jnp.einsum(
        "fns,fne->fse", place, stale_grad, preferred_element_type=jnp.float32
    ).astype(jnp.bfloat16)
    send_rows = (
        jnp.full((local_feats, grad_total), rows_per_shard, jnp.int32)
        .at[which_feature, grad_slot]
        .set(grad_row)
    )
    recv_grads = lax.all_to_all(
        send_grads.reshape(local_feats, peers, grad_cap, width),
        "dp",
        split_axis=1,
        concat_axis=1,
        tiled=True,
    )
    recv_rows = lax.all_to_all(
        send_rows.reshape(local_feats, peers, grad_cap),
        "dp",
        split_axis=1,
        concat_axis=1,
        tiled=True,
    )
    landing = selection_matrix(recv_rows.reshape(local_feats, grad_total), rows_per_shard)
    summed = jnp.einsum(
        "wjc,wjl->wcl",
        landing,
        recv_grads.reshape(local_feats, grad_total, width),
        preferred_element_type=jnp.float32,
    )
    new_accum = accum + jnp.mean(summed * summed, axis=2)
    new_table = embed_table - learn_rate * summed / jnp.sqrt(new_accum)[:, :, None]
    batch_dev = bag_len.shape[1]
    look_dev = lookup_row.shape[1]
    bag_size = look_dev // batch_dev
    look_cap = max(2, 2 * look_dev // peers)
    look_total = peers * look_cap
    look_slot = bucket_slots(lookup_owner[:, :, 0], look_cap, peers)
    wanted = (
        jnp.zeros((local_feats, look_total), jnp.int32).at[which_feature, look_slot].set(lookup_row)
    )
    requested_ids = lax.all_to_all(
        wanted.reshape(local_feats, peers, look_cap), "dp", split_axis=1, concat_axis=1, tiled=True
    ).reshape(local_feats, look_total)
    second_table = embed_table.astype(jnp.bfloat16)
    served = jnp.einsum(
        "adv,avm->adm",
        selection_matrix(requested_ids, rows_per_shard),
        second_table,
        preferred_element_type=jnp.float32,
    ).astype(jnp.bfloat16)
    returned = lax.all_to_all(
        served.reshape(local_feats, peers, look_cap, width),
        "dp",
        split_axis=1,
        concat_axis=1,
        tiled=True,
    ).reshape(local_feats, look_total, width)
    slots = look_slot.reshape(local_feats, batch_dev, bag_size)
    mixing = jnp.zeros((local_feats, batch_dev, look_total), jnp.bfloat16)
    for member in range(bag_size):
        used = (bag_len > member).astype(jnp.bfloat16)
        mixing = mixing + selection_matrix(slots[:, :, member], look_total) * used[:, :, None]
    pooled = jnp.einsum(
        "fbs,fse->fbe", mixing, returned, preferred_element_type=jnp.float32
    ).astype(jnp.bfloat16)
    start = jnp.transpose(pooled, (1, 0, 2)).reshape(batch_dev, local_feats * width)
    start_f = start.astype(jnp.float32)
    n_layers = up_factor_weight.shape[0]
    state = start
    states = []
    downs = []
    crosses = []
    for layer in range(n_layers):
        down_sum = cross_down(state, v_weight[layer])
        cross_out = (
            jnp.dot(down_sum, up_factor_weight[layer], preferred_element_type=jnp.float32)
            + cross_bias[layer]
        )
        states.append(state)
        downs.append(down_sum)
        crosses.append(cross_out)
        state = (start_f * cross_out + state.astype(jnp.float32)).astype(jnp.bfloat16)
    logit = lax.psum(jnp.sum(state.astype(jnp.float32) * head_weight[None, :], axis=1), "mp")
    slope = (jax.nn.sigmoid(logit) - label.astype(jnp.float32)) / jnp.sqrt(
        jnp.float32(batch_dev * peers)
    )
    upstream = slope[:, None] * head_weight[None, :]
    head_grad = jnp.sum(slope[:, None] * state.astype(jnp.float32), axis=0)
    to_start = jnp.zeros(start_f.shape, jnp.float32)
    grads_u = [None] * n_layers
    grads_v = [None] * n_layers
    bias_grads = [None] * n_layers
    for layer in reversed(range(n_layers)):
        direct = upstream * start_f
        bias_grads[layer] = jnp.sum(direct, axis=0)
        direct_bias_term = direct.astype(jnp.bfloat16)
        grad_u_layer = contract_first(downs[layer], direct_bias_term)
        back_sum = over_copies(
            contract_last(direct_bias_term, up_factor_weight[layer]), "mp"
        ).astype(jnp.bfloat16)
        down_factor_gradient = contract_first(back_sum, states[layer])
        to_start = to_start + upstream * crosses[layer]
        upstream = upstream + jnp.dot(back_sum, v_weight[layer], preferred_element_type=jnp.float32)
        grads_u[layer] = grad_u_layer
        grads_v[layer] = down_factor_gradient
    grad_u = jnp.stack(grads_u)
    grad_v = jnp.stack(grads_v)
    grad_u, grad_v = side_by_side((grad_u, grad_v), "dp", 1, 0)
    grad_small = butterfly_sum(jnp.stack(bias_grads + [head_grad]), "dp")
    grad_pooled = (upstream + to_start).astype(jnp.bfloat16)
    return (new_table, new_accum, grad_u, grad_v, grad_small, grad_pooled)


def solution(mesh):
    return jax.shard_map(
        local,
        mesh=mesh,
        in_specs=(
            P("mp", "dp", None),
            P("mp", "dp"),
            P("mp", "dp", None),
            P("mp", "dp", None),
            P("mp", "dp"),
            P("mp", "dp", None),
            P("mp", "dp"),
            P("mp", "dp"),
            P("dp"),
            P(None, None, "mp"),
            P(None, None, "mp"),
            P(None, "mp"),
            P("mp"),
        ),
        out_specs=(
            P("mp", "dp", None),
            P("mp", "dp"),
            P(None, "dp", "mp"),
            P(None, "dp", "mp"),
            P(None, "mp"),
            P("dp", "mp"),
        ),
        check_vma=False,
    )
```

```python
import jax
import jax.numpy as jnp
from jax import lax
from jax.sharding import PartitionSpec as P

learn_rate = 0.5


def in_blocks(array, dim, devices):
    shape = array.shape
    parts = array.reshape(*shape[:dim], devices, shape[dim] // devices, *shape[dim + 1 :])
    return jnp.moveaxis(parts, dim, 0)


def sum_at_owner(array, axis, dim):
    parts = in_blocks(array, dim, lax.axis_size(axis))
    arrived = lax.all_to_all(parts, axis, split_axis=0, concat_axis=0, tiled=True)
    return arrived.sum(axis=0)


def copy_for_each(array, axis):
    copies = jnp.broadcast_to(array, (lax.axis_size(axis), *array.shape))
    return lax.all_to_all(copies, axis, split_axis=0, concat_axis=0, tiled=True)


def over_copies(array, axis):
    return copy_for_each(array, axis).sum(axis=0)


def butterfly_sum(array, axis):
    peers = lax.axis_size(axis)
    step = 1
    while step < peers:
        array = array + lax.ppermute(array, axis, [(i, i ^ step) for i in range(peers)])
        step *= 2
    return array


def side_by_side(arrays, axis, dim, along):
    widths = [a.shape[along] for a in arrays]
    both = jnp.concatenate(arrays, axis=along)
    filled = lax.psum_scatter(both, axis, scatter_dimension=dim, tiled=True)
    return tuple(jnp.split(filled, [sum(widths[:k]) for k in range(1, len(widths))], axis=along))


def bucket_slots(owners, capacity, peers):
    count = owners.shape[1]
    onehot = (owners[:, None, :] == jnp.arange(peers)[None, :, None]).astype(jnp.bfloat16)
    earlier = (jnp.arange(count)[:, None] < jnp.arange(count)[None, :]).astype(jnp.bfloat16)
    before = jnp.einsum("fpi,ij->fpj", onehot, earlier, preferred_element_type=jnp.float32)
    order_in = jnp.sum(before * onehot.astype(jnp.float32), axis=1)
    return owners * capacity + order_in.astype(jnp.int32)


def selection_matrix(indices, length):
    return (indices[:, :, None] == jnp.arange(length)[None, None, :]).astype(jnp.bfloat16)


def contract_last(left, right):
    return lax.dot_general(
        left, right, (((1,), (1,)), ((), ())), preferred_element_type=jnp.float32
    )


def contract_first(left, right):
    return lax.dot_general(
        left, right, (((0,), (0,)), ((), ())), preferred_element_type=jnp.float32
    )


def cross_down(state, v_layer):
    share = sum_at_owner(contract_last(state, v_layer), "mp", 0)
    return lax.all_gather(share.astype(jnp.bfloat16), "mp", axis=0, tiled=True)


def local(
    embed_table,
    accum,
    stale_grad,
    grad_owner,
    grad_row,
    lookup_owner,
    lookup_row,
    bag_len,
    label,
    up_factor_weight,
    v_weight,
    cross_bias,
    head_weight,
):
    peers = lax.axis_size("dp")
    local_feats, grad_dev, width = stale_grad.shape
    rows_per_shard = embed_table.shape[1]
    which_feature = jnp.arange(local_feats)[:, None]
    grad_cap = max(2, 2 * grad_dev // peers)
    grad_total = peers * grad_cap
    grad_slot = bucket_slots(grad_owner[:, :, 0], grad_cap, peers)
    place = selection_matrix(grad_slot, grad_total)
    send_grads = jnp.einsum(
        "fns,fne->fse", place, stale_grad, preferred_element_type=jnp.float32
    ).astype(jnp.bfloat16)
    send_rows = (
        jnp.full((local_feats, grad_total), rows_per_shard, jnp.int32)
        .at[which_feature, grad_slot]
        .set(grad_row)
    )
    recv_grads = lax.all_to_all(
        send_grads.reshape(local_feats, peers, grad_cap, width),
        "dp",
        split_axis=1,
        concat_axis=1,
        tiled=True,
    )
    recv_rows = lax.all_to_all(
        send_rows.reshape(local_feats, peers, grad_cap),
        "dp",
        split_axis=1,
        concat_axis=1,
        tiled=True,
    )
    landing = selection_matrix(recv_rows.reshape(local_feats, grad_total), rows_per_shard)
    summed = jnp.einsum(
        "wjc,wjl->wcl",
        landing,
        recv_grads.reshape(local_feats, grad_total, width),
        preferred_element_type=jnp.float32,
    )
    new_accum = accum + jnp.mean(summed * summed, axis=2)
    new_table = embed_table - learn_rate * summed / jnp.sqrt(new_accum)[:, :, None]
    batch_dev = bag_len.shape[1]
    look_dev = lookup_row.shape[1]
    bag_size = look_dev // batch_dev
    look_cap = max(2, 2 * look_dev // peers)
    look_total = peers * look_cap
    look_slot = bucket_slots(lookup_owner[:, :, 0], look_cap, peers)
    wanted = (
        jnp.zeros((local_feats, look_total), jnp.int32).at[which_feature, look_slot].set(lookup_row)
    )
    requested_ids = lax.all_to_all(
        wanted.reshape(local_feats, peers, look_cap), "dp", split_axis=1, concat_axis=1, tiled=True
    ).reshape(local_feats, look_total)
    second_table = embed_table.astype(jnp.bfloat16)
    served = jnp.einsum(
        "adv,avm->adm",
        selection_matrix(requested_ids, rows_per_shard),
        second_table,
        preferred_element_type=jnp.float32,
    ).astype(jnp.bfloat16)
    returned = lax.all_to_all(
        served.reshape(local_feats, peers, look_cap, width),
        "dp",
        split_axis=1,
        concat_axis=1,
        tiled=True,
    ).reshape(local_feats, look_total, width)
    slots = look_slot.reshape(local_feats, batch_dev, bag_size)
    mixing = jnp.zeros((local_feats, batch_dev, look_total), jnp.bfloat16)
    for member in range(bag_size):
        used = (bag_len > member).astype(jnp.bfloat16)
        mixing = mixing + selection_matrix(slots[:, :, member], look_total) * used[:, :, None]
    pooled = jnp.einsum(
        "fbs,fse->fbe", mixing, returned, preferred_element_type=jnp.float32
    ).astype(jnp.bfloat16)
    start = jnp.transpose(pooled, (1, 0, 2)).reshape(batch_dev, local_feats * width)
    start_f = start.astype(jnp.float32)
    n_layers = up_factor_weight.shape[0]
    state = start
    states = []
    downs = []
    crosses = []
    for layer in range(n_layers):
        down_sum = cross_down(state, v_weight[layer])
        cross_out = (
            jnp.dot(down_sum, up_factor_weight[layer], preferred_element_type=jnp.float32)
            + cross_bias[layer]
        )
        states.append(state)
        downs.append(down_sum)
        crosses.append(cross_out)
        state = (start_f * cross_out + state.astype(jnp.float32)).astype(jnp.bfloat16)
    logit = lax.psum(jnp.sum(state.astype(jnp.float32) * head_weight[None, :], axis=1), "mp")
    slope = (jax.nn.sigmoid(logit) - label.astype(jnp.float32)) / jnp.sqrt(
        jnp.float32(batch_dev * peers)
    )
    upstream = slope[:, None] * head_weight[None, :]
    head_grad = jnp.sum(slope[:, None] * state.astype(jnp.float32), axis=0)
    to_start = jnp.zeros(start_f.shape, jnp.float32)
    grads_u = [None] * n_layers
    grads_v = [None] * n_layers
    bias_grads = [None] * n_layers
    for layer in reversed(range(n_layers)):
        direct = upstream * start_f
        bias_grads[layer] = jnp.sum(direct, axis=0)
        direct_bias_term = direct.astype(jnp.bfloat16)
        grad_u_layer = contract_first(downs[layer], direct_bias_term)
        back_sum = over_copies(
            contract_last(direct_bias_term, up_factor_weight[layer]), "mp"
        ).astype(jnp.bfloat16)
        if layer == n_layers - 1:
            halves = jnp.swapaxes(grad_u_layer.reshape(grad_u_layer.shape[0], 2, -1), 0, 1)
            early_u = lax.psum_scatter(halves, "dp", scatter_dimension=1, tiled=True)
        else:
            early_u, back_sum = lax.optimization_barrier((early_u, back_sum))
        down_factor_gradient = contract_first(back_sum, states[layer])
        to_start = to_start + upstream * crosses[layer]
        upstream = upstream + jnp.dot(back_sum, v_weight[layer], preferred_element_type=jnp.float32)
        grads_u[layer] = grad_u_layer
        grads_v[layer] = down_factor_gradient
    rest = lax.psum_scatter(
        jnp.stack((grads_u[0], grads_v[0], grads_v[1])), "dp", scatter_dimension=1, tiled=True
    )
    early_u = jnp.swapaxes(early_u, 0, 1).reshape(1, early_u.shape[1], -1)
    grad_u = jnp.concatenate((rest[0:1], early_u), axis=0)
    grad_v = rest[1:3]
    grad_small = butterfly_sum(jnp.stack(bias_grads + [head_grad]), "dp")
    grad_pooled = (upstream + to_start).astype(jnp.bfloat16)
    return (new_table, new_accum, grad_u, grad_v, grad_small, grad_pooled)


def solution(mesh):
    return jax.shard_map(
        local,
        mesh=mesh,
        in_specs=(
            P("mp", "dp", None),
            P("mp", "dp"),
            P("mp", "dp", None),
            P("mp", "dp", None),
            P("mp", "dp"),
            P("mp", "dp", None),
            P("mp", "dp"),
            P("mp", "dp"),
            P("dp"),
            P(None, None, "mp"),
            P(None, None, "mp"),
            P(None, "mp"),
            P("mp"),
        ),
        out_specs=(
            P("mp", "dp", None),
            P("mp", "dp"),
            P(None, "dp", "mp"),
            P(None, "dp", "mp"),
            P(None, "mp"),
            P("dp", "mp"),
        ),
        check_vma=False,
    )
```

```python
import functools

import jax
import jax.numpy as jnp
import numpy as np
from jax import lax
from jax.sharding import PartitionSpec as P

learn_rate = 0.5


def in_blocks(array, dim, devices):
    shape = array.shape
    parts = array.reshape(*shape[:dim], devices, shape[dim] // devices, *shape[dim + 1 :])
    return jnp.moveaxis(parts, dim, 0)


def sum_at_owner(array, axis, dim):
    parts = in_blocks(array, dim, lax.axis_size(axis))
    arrived = lax.all_to_all(parts, axis, split_axis=0, concat_axis=0, tiled=True)
    return arrived.sum(axis=0)


def copy_for_each(array, axis):
    copies = jnp.broadcast_to(array, (lax.axis_size(axis), *array.shape))
    return lax.all_to_all(copies, axis, split_axis=0, concat_axis=0, tiled=True)


def over_copies(array, axis):
    return copy_for_each(array, axis).sum(axis=0)


def ring_sum_scatter(blocks, axis, stride):
    size = blocks.shape[0]
    peers = lax.axis_size(axis)
    pos = (lax.axis_index(axis) // stride) % size
    ahead = [
        (i, i + (((i // stride) % size + 1) % size - (i // stride) % size) * stride)
        for i in range(peers)
    ]
    carry = blocks[(pos + size - 1) % size]
    for step in range(size - 1):
        carry = lax.ppermute(carry, axis, ahead) + blocks[(pos + 2 * size - step - 2) % size]
    return carry

def tree_sum_scatter(array, axis, dim, splits):
    lead = array.shape[:dim]
    parts = array.reshape(*lead, *splits, array.shape[dim] // np.prod(splits), *array.shape[dim + 1:])
    stride = 1
    for level in reversed(range(len(splits))):
        parts = jnp.moveaxis(parts, dim + level, 0)
        parts = ring_sum_scatter(parts, axis, stride)
        stride *= splits[level]
    return parts

def side_by_side(arrays, axis, dim, along):
    widths = [a.shape[along] for a in arrays]
    both = jnp.concatenate(arrays, axis=along)
    filled = lax.psum_scatter(both, axis, scatter_dimension=dim, tiled=True)
    return tuple(jnp.split(filled, [sum(widths[:k]) for k in range(1, len(widths))], axis=along))


def bucket_slots(owners, capacity, peers):
    count = owners.shape[1]
    onehot = (owners[:, None, :] == jnp.arange(peers)[None, :, None]).astype(jnp.bfloat16)
    earlier = (jnp.arange(count)[:, None] < jnp.arange(count)[None, :]).astype(jnp.bfloat16)
    before = jnp.einsum("fpi,ij->fpj", onehot, earlier, preferred_element_type=jnp.float32)
    order_in = jnp.sum(before * onehot.astype(jnp.float32), axis=1)
    return owners * capacity + order_in.astype(jnp.int32)


def selection_matrix(indices, length):
    return (indices[:, :, None] == jnp.arange(length)[None, None, :]).astype(jnp.bfloat16)


def contract_last(left, right):
    return lax.dot_general(
        left, right, (((1,), (1,)), ((), ())), preferred_element_type=jnp.float32
    )


def contract_first(left, right):
    return lax.dot_general(
        left, right, (((0,), (0,)), ((), ())), preferred_element_type=jnp.float32
    )


def cross_down(state, v_layer):
    share = sum_at_owner(contract_last(state, v_layer), "mp", 0)
    return lax.all_gather(share.astype(jnp.bfloat16), "mp", axis=0, tiled=True)


def dp_factors(mesh):
    column = mesh.devices[:, 0]
    try:
        keys = [(d.coords[2], d.coords[0], d.core_on_chip) for d in column]
    except AttributeError:
        return (len(column),)
    factors = tuple(len(set(k[level] for k in keys)) for level in range(3))
    if int(np.prod(factors)) != len(column) or keys != sorted(keys):
        return (len(column),)
    return factors


def local(
    splits,
    embed_table,
    accum,
    stale_grad,
    grad_owner,
    grad_row,
    lookup_owner,
    lookup_row,
    bag_len,
    label,
    up_factor_weight,
    v_weight,
    cross_bias,
    head_weight,
):
    peers = lax.axis_size("dp")
    local_feats, grad_dev, width = stale_grad.shape
    rows_per_shard = embed_table.shape[1]
    which_feature = jnp.arange(local_feats)[:, None]
    grad_cap = max(2, 2 * grad_dev // peers)
    grad_total = peers * grad_cap
    grad_slot = bucket_slots(grad_owner[:, :, 0], grad_cap, peers)
    place = selection_matrix(grad_slot, grad_total)
    send_grads = jnp.einsum(
        "fns,fne->fse", place, stale_grad, preferred_element_type=jnp.float32
    ).astype(jnp.bfloat16)
    send_rows = (
        jnp.full((local_feats, grad_total), rows_per_shard, jnp.int32)
        .at[which_feature, grad_slot]
        .set(grad_row)
    )
    recv_grads = lax.all_to_all(
        send_grads.reshape(local_feats, peers, grad_cap, width),
        "dp",
        split_axis=1,
        concat_axis=1,
        tiled=True,
    )
    recv_rows = lax.all_to_all(
        send_rows.reshape(local_feats, peers, grad_cap),
        "dp",
        split_axis=1,
        concat_axis=1,
        tiled=True,
    )
    landing = selection_matrix(recv_rows.reshape(local_feats, grad_total), rows_per_shard)
    summed = jnp.einsum(
        "wjc,wjl->wcl",
        landing,
        recv_grads.reshape(local_feats, grad_total, width),
        preferred_element_type=jnp.float32,
    )
    new_accum = accum + jnp.mean(summed * summed, axis=2)
    new_table = embed_table - learn_rate * summed / jnp.sqrt(new_accum)[:, :, None]
    batch_dev = bag_len.shape[1]
    look_dev = lookup_row.shape[1]
    bag_size = look_dev // batch_dev
    look_cap = max(2, 2 * look_dev // peers)
    look_total = peers * look_cap
    look_slot = bucket_slots(lookup_owner[:, :, 0], look_cap, peers)
    wanted = (
        jnp.zeros((local_feats, look_total), jnp.int32).at[which_feature, look_slot].set(lookup_row)
    )
    requested_ids = lax.all_to_all(
        wanted.reshape(local_feats, peers, look_cap), "dp", split_axis=1, concat_axis=1, tiled=True
    ).reshape(local_feats, look_total)
    second_table = embed_table.astype(jnp.bfloat16)
    served = jnp.einsum(
        "adv,avm->adm",
        selection_matrix(requested_ids, rows_per_shard),
        second_table,
        preferred_element_type=jnp.float32,
    ).astype(jnp.bfloat16)
    returned = lax.all_to_all(
        served.reshape(local_feats, peers, look_cap, width),
        "dp",
        split_axis=1,
        concat_axis=1,
        tiled=True,
    ).reshape(local_feats, look_total, width)
    slots = look_slot.reshape(local_feats, batch_dev, bag_size)
    mixing = jnp.zeros((local_feats, batch_dev, look_total), jnp.bfloat16)
    for member in range(bag_size):
        used = (bag_len > member).astype(jnp.bfloat16)
        mixing = mixing + selection_matrix(slots[:, :, member], look_total) * used[:, :, None]
    pooled = jnp.einsum(
        "fbs,fse->fbe", mixing, returned, preferred_element_type=jnp.float32
    ).astype(jnp.bfloat16)
    start = jnp.transpose(pooled, (1, 0, 2)).reshape(batch_dev, local_feats * width)
    start_f = start.astype(jnp.float32)
    n_layers = up_factor_weight.shape[0]
    state = start
    states = []
    downs = []
    crosses = []
    for layer in range(n_layers):
        down_sum = cross_down(state, v_weight[layer])
        cross_out = (
            jnp.dot(down_sum, up_factor_weight[layer], preferred_element_type=jnp.float32)
            + cross_bias[layer]
        )
        states.append(state)
        downs.append(down_sum)
        crosses.append(cross_out)
        state = (start_f * cross_out + state.astype(jnp.float32)).astype(jnp.bfloat16)
    logit = lax.psum(jnp.sum(state.astype(jnp.float32) * head_weight[None, :], axis=1), "mp")
    slope = (jax.nn.sigmoid(logit) - label.astype(jnp.float32)) / jnp.sqrt(
        jnp.float32(batch_dev * peers)
    )
    upstream = slope[:, None] * head_weight[None, :]
    head_grad = jnp.sum(slope[:, None] * state.astype(jnp.float32), axis=0)
    to_start = jnp.zeros(start_f.shape, jnp.float32)
    grads_u = [None] * n_layers
    grads_v = [None] * n_layers
    bias_grads = [None] * n_layers
    for layer in reversed(range(n_layers)):
        direct = upstream * start_f
        bias_grads[layer] = jnp.sum(direct, axis=0)
        direct_bias_term = direct.astype(jnp.bfloat16)
        grad_u_layer = contract_first(downs[layer], direct_bias_term)
        back_sum = over_copies(
            contract_last(direct_bias_term, up_factor_weight[layer]), "mp"
        ).astype(jnp.bfloat16)
        down_factor_gradient = contract_first(back_sum, states[layer])
        to_start = to_start + upstream * crosses[layer]
        upstream = upstream + jnp.dot(back_sum, v_weight[layer], preferred_element_type=jnp.float32)
        grads_u[layer] = grad_u_layer
        grads_v[layer] = down_factor_gradient
    both = jnp.concatenate((jnp.stack(grads_u), jnp.stack(grads_v)), axis=0)
    grad_u, grad_v = jnp.split(tree_sum_scatter(both, "dp", 1, splits), 2, axis=0)
    grad_small = over_copies(jnp.stack(bias_grads + [head_grad]), "dp")
    grad_pooled = (upstream + to_start).astype(jnp.bfloat16)
    return (new_table, new_accum, grad_u, grad_v, grad_small, grad_pooled)


def solution(mesh):
    return jax.shard_map(
        functools.partial(local, dp_factors(mesh)),
        mesh=mesh,
        in_specs=(
            P("mp", "dp", None),
            P("mp", "dp"),
            P("mp", "dp", None),
            P("mp", "dp", None),
            P("mp", "dp"),
            P("mp", "dp", None),
            P("mp", "dp"),
            P("mp", "dp"),
            P("dp"),
            P(None, None, "mp"),
            P(None, None, "mp"),
            P(None, "mp"),
            P("mp"),
        ),
        out_specs=(
            P("mp", "dp", None),
            P("mp", "dp"),
            P(None, "dp", "mp"),
            P(None, "dp", "mp"),
            P(None, "mp"),
            P("dp", "mp"),
        ),
        check_vma=False,
    )
```

```python
import functools

import jax
import jax.numpy as jnp
import numpy as np
from jax import lax
from jax.sharding import PartitionSpec as P

learn_rate = 0.5


def in_blocks(array, dim, devices):
    shape = array.shape
    parts = array.reshape(*shape[:dim], devices, shape[dim] // devices, *shape[dim + 1 :])
    return jnp.moveaxis(parts, dim, 0)


def sum_at_owner(array, axis, dim):
    parts = in_blocks(array, dim, lax.axis_size(axis))
    arrived = lax.all_to_all(parts, axis, split_axis=0, concat_axis=0, tiled=True)
    return arrived.sum(axis=0)


def copy_for_each(array, axis):
    copies = jnp.broadcast_to(array, (lax.axis_size(axis), *array.shape))
    return lax.all_to_all(copies, axis, split_axis=0, concat_axis=0, tiled=True)


def over_copies(array, axis):
    return copy_for_each(array, axis).sum(axis=0)


def ring_sum_scatter(blocks, axis, stride, wire):
    size = blocks.shape[0]
    peers = lax.axis_size(axis)
    pos = (lax.axis_index(axis) // stride) % size
    ahead = [
        (i, i + (((i // stride) % size + 1) % size - (i // stride) % size) * stride)
        for i in range(peers)
    ]
    carry = blocks[(pos + size - 1) % size]
    for step in range(size - 1):
        arrived = lax.ppermute(carry.astype(wire), axis, ahead).astype(carry.dtype)
        carry = arrived + blocks[(pos + 2 * size - step - 2) % size]
    return carry

def tree_sum_scatter(array, axis, dim, splits, wires):
    lead = array.shape[:dim]
    parts = array.reshape(*lead, *splits, array.shape[dim] // np.prod(splits), *array.shape[dim + 1:])
    stride = 1
    for level in reversed(range(len(splits))):
        parts = jnp.moveaxis(parts, dim + level, 0)
        parts = ring_sum_scatter(parts, axis, stride, wires[level])
        stride *= splits[level]
    return parts

def butterfly_sum(array, axis):
    peers = lax.axis_size(axis)
    step = 1
    while step < peers:
        array = array + lax.ppermute(array, axis, [(i, i ^ step) for i in range(peers)])
        step *= 2
    return array


def side_by_side(arrays, axis, dim, along):
    widths = [a.shape[along] for a in arrays]
    both = jnp.concatenate(arrays, axis=along)
    filled = lax.psum_scatter(both, axis, scatter_dimension=dim, tiled=True)
    return tuple(jnp.split(filled, [sum(widths[:k]) for k in range(1, len(widths))], axis=along))


def bucket_slots(owners, capacity, peers):
    count = owners.shape[1]
    onehot = (owners[:, None, :] == jnp.arange(peers)[None, :, None]).astype(jnp.bfloat16)
    earlier = (jnp.arange(count)[:, None] < jnp.arange(count)[None, :]).astype(jnp.bfloat16)
    before = jnp.einsum("fpi,ij->fpj", onehot, earlier, preferred_element_type=jnp.float32)
    order_in = jnp.sum(before * onehot.astype(jnp.float32), axis=1)
    return owners * capacity + order_in.astype(jnp.int32)


def selection_matrix(indices, length):
    return (indices[:, :, None] == jnp.arange(length)[None, None, :]).astype(jnp.bfloat16)


def contract_last(left, right):
    return lax.dot_general(
        left, right, (((1,), (1,)), ((), ())), preferred_element_type=jnp.float32
    )


def contract_first(left, right):
    return lax.dot_general(
        left, right, (((0,), (0,)), ((), ())), preferred_element_type=jnp.float32
    )


def cross_down(state, v_layer):
    share = sum_at_owner(contract_last(state, v_layer), "mp", 0)
    return lax.all_gather(share.astype(jnp.bfloat16), "mp", axis=0, tiled=True)


def dp_factors(mesh):
    column = mesh.devices[:, 0]
    try:
        keys = [(d.coords[2], d.coords[0], d.core_on_chip) for d in column]
    except AttributeError:
        return (len(column),)
    factors = tuple(len(set(k[level] for k in keys)) for level in range(3))
    if int(np.prod(factors)) != len(column) or keys != sorted(keys):
        return (len(column),)
    return factors


def local(
    splits,
    embed_table,
    accum,
    stale_grad,
    grad_owner,
    grad_row,
    lookup_owner,
    lookup_row,
    bag_len,
    label,
    up_factor_weight,
    v_weight,
    cross_bias,
    head_weight,
):
    peers = lax.axis_size("dp")
    local_feats, grad_dev, width = stale_grad.shape
    rows_per_shard = embed_table.shape[1]
    which_feature = jnp.arange(local_feats)[:, None]
    grad_cap = max(2, 2 * grad_dev // peers)
    grad_total = peers * grad_cap
    grad_slot = bucket_slots(grad_owner[:, :, 0], grad_cap, peers)
    place = selection_matrix(grad_slot, grad_total)
    send_grads = jnp.einsum(
        "fns,fne->fse", place, stale_grad, preferred_element_type=jnp.float32
    ).astype(jnp.bfloat16)
    send_rows = (
        jnp.full((local_feats, grad_total), rows_per_shard, jnp.int32)
        .at[which_feature, grad_slot]
        .set(grad_row)
    )
    recv_grads = lax.all_to_all(
        send_grads.reshape(local_feats, peers, grad_cap, width),
        "dp",
        split_axis=1,
        concat_axis=1,
        tiled=True,
    )
    recv_rows = lax.all_to_all(
        send_rows.reshape(local_feats, peers, grad_cap),
        "dp",
        split_axis=1,
        concat_axis=1,
        tiled=True,
    )
    landing = selection_matrix(recv_rows.reshape(local_feats, grad_total), rows_per_shard)
    summed = jnp.einsum(
        "wjc,wjl->wcl",
        landing,
        recv_grads.reshape(local_feats, grad_total, width),
        preferred_element_type=jnp.float32,
    )
    new_accum = accum + jnp.mean(summed * summed, axis=2)
    new_table = embed_table - learn_rate * summed / jnp.sqrt(new_accum)[:, :, None]
    batch_dev = bag_len.shape[1]
    look_dev = lookup_row.shape[1]
    bag_size = look_dev // batch_dev
    look_cap = max(2, 2 * look_dev // peers)
    look_total = peers * look_cap
    look_slot = bucket_slots(lookup_owner[:, :, 0], look_cap, peers)
    wanted = (
        jnp.zeros((local_feats, look_total), jnp.int32).at[which_feature, look_slot].set(lookup_row)
    )
    requested_ids = lax.all_to_all(
        wanted.reshape(local_feats, peers, look_cap), "dp", split_axis=1, concat_axis=1, tiled=True
    ).reshape(local_feats, look_total)
    second_table = embed_table.astype(jnp.bfloat16)
    served = jnp.einsum(
        "adv,avm->adm",
        selection_matrix(requested_ids, rows_per_shard),
        second_table,
        preferred_element_type=jnp.float32,
    ).astype(jnp.bfloat16)
    returned = lax.all_to_all(
        served.reshape(local_feats, peers, look_cap, width),
        "dp",
        split_axis=1,
        concat_axis=1,
        tiled=True,
    ).reshape(local_feats, look_total, width)
    slots = look_slot.reshape(local_feats, batch_dev, bag_size)
    mixing = jnp.zeros((local_feats, batch_dev, look_total), jnp.bfloat16)
    for member in range(bag_size):
        used = (bag_len > member).astype(jnp.bfloat16)
        mixing = mixing + selection_matrix(slots[:, :, member], look_total) * used[:, :, None]
    pooled = jnp.einsum(
        "fbs,fse->fbe", mixing, returned, preferred_element_type=jnp.float32
    ).astype(jnp.bfloat16)
    start = jnp.transpose(pooled, (1, 0, 2)).reshape(batch_dev, local_feats * width)
    start_f = start.astype(jnp.float32)
    n_layers = up_factor_weight.shape[0]
    state = start
    states = []
    downs = []
    crosses = []
    for layer in range(n_layers):
        down_sum = cross_down(state, v_weight[layer])
        cross_out = (
            jnp.dot(down_sum, up_factor_weight[layer], preferred_element_type=jnp.float32)
            + cross_bias[layer]
        )
        states.append(state)
        downs.append(down_sum)
        crosses.append(cross_out)
        state = (start_f * cross_out + state.astype(jnp.float32)).astype(jnp.bfloat16)
    logit = lax.psum(jnp.sum(state.astype(jnp.float32) * head_weight[None, :], axis=1), "mp")
    slope = (jax.nn.sigmoid(logit) - label.astype(jnp.float32)) / jnp.sqrt(
        jnp.float32(batch_dev * peers)
    )
    upstream = slope[:, None] * head_weight[None, :]
    head_grad = jnp.sum(slope[:, None] * state.astype(jnp.float32), axis=0)
    to_start = jnp.zeros(start_f.shape, jnp.float32)
    grads_u = [None] * n_layers
    grads_v = [None] * n_layers
    bias_grads = [None] * n_layers
    for layer in reversed(range(n_layers)):
        direct = upstream * start_f
        bias_grads[layer] = jnp.sum(direct, axis=0)
        direct_bias_term = direct.astype(jnp.bfloat16)
        grad_u_layer = contract_first(downs[layer], direct_bias_term)
        back_sum = over_copies(
            contract_last(direct_bias_term, up_factor_weight[layer]), "mp"
        ).astype(jnp.bfloat16)
        down_factor_gradient = contract_first(back_sum, states[layer])
        to_start = to_start + upstream * crosses[layer]
        upstream = upstream + jnp.dot(back_sum, v_weight[layer], preferred_element_type=jnp.float32)
        grads_u[layer] = grad_u_layer
        grads_v[layer] = down_factor_gradient
    both = jnp.concatenate((jnp.stack(grads_u), jnp.stack(grads_v)), axis=0)
    wires = [jnp.float32] + [jnp.bfloat16] * (len(splits) - 1)
    grad_u, grad_v = jnp.split(tree_sum_scatter(both, "dp", 1, splits, wires), 2, axis=0)
    grad_small = butterfly_sum(jnp.stack(bias_grads + [head_grad]), "dp")
    grad_pooled = (upstream + to_start).astype(jnp.bfloat16)
    return (new_table, new_accum, grad_u, grad_v, grad_small, grad_pooled)


def solution(mesh):
    return jax.shard_map(
        functools.partial(local, dp_factors(mesh)),
        mesh=mesh,
        in_specs=(
            P("mp", "dp", None),
            P("mp", "dp"),
            P("mp", "dp", None),
            P("mp", "dp", None),
            P("mp", "dp"),
            P("mp", "dp", None),
            P("mp", "dp"),
            P("mp", "dp"),
            P("dp"),
            P(None, None, "mp"),
            P(None, None, "mp"),
            P(None, "mp"),
            P("mp"),
        ),
        out_specs=(
            P("mp", "dp", None),
            P("mp", "dp"),
            P(None, "dp", "mp"),
            P(None, "dp", "mp"),
            P(None, "mp"),
            P("dp", "mp"),
        ),
        check_vma=False,
    )
```

```python
import functools

import jax
import jax.numpy as jnp
import numpy as np
from jax import lax
from jax.sharding import PartitionSpec as P

learn_rate = 0.5


def in_blocks(array, dim, devices):
    shape = array.shape
    parts = array.reshape(*shape[:dim], devices, shape[dim] // devices, *shape[dim + 1 :])
    return jnp.moveaxis(parts, dim, 0)


def sum_at_owner(array, axis, dim):
    parts = in_blocks(array, dim, lax.axis_size(axis))
    arrived = lax.all_to_all(parts, axis, split_axis=0, concat_axis=0, tiled=True)
    return arrived.sum(axis=0)


def copy_for_each(array, axis):
    copies = jnp.broadcast_to(array, (lax.axis_size(axis), *array.shape))
    return lax.all_to_all(copies, axis, split_axis=0, concat_axis=0, tiled=True)


def over_copies(array, axis):
    return copy_for_each(array, axis).sum(axis=0)


def ring_sum_scatter(blocks, axis, stride, wire):
    size = blocks.shape[0]
    peers = lax.axis_size(axis)
    pos = (lax.axis_index(axis) // stride) % size
    ahead = [
        (i, i + (((i // stride) % size + 1) % size - (i // stride) % size) * stride)
        for i in range(peers)
    ]
    carry = blocks[(pos + size - 1) % size]
    for step in range(size - 1):
        arrived = lax.ppermute(carry.astype(wire), axis, ahead).astype(carry.dtype)
        carry = arrived + blocks[(pos + 2 * size - step - 2) % size]
    return carry

def direct_sum_scatter(blocks, axis, stride, wire):
    size = blocks.shape[0]
    peers = lax.axis_size(axis)
    pos = (lax.axis_index(axis) // stride) % size
    total = blocks[pos]
    for offset in range(1, size):
        toward = [
            (i, i + (((i // stride) % size + offset) % size - (i // stride) % size) * stride)
            for i in range(peers)
        ]
        sent = blocks[(pos + offset) % size].astype(wire)
        total = total + lax.ppermute(sent, axis, toward).astype(total.dtype)
    return total


def tree_sum_scatter(array, axis, dim, splits, wires):
    lead = array.shape[:dim]
    parts = array.reshape(*lead, *splits, array.shape[dim] // np.prod(splits), *array.shape[dim + 1:])
    stride = 1
    for level in reversed(range(len(splits))):
        parts = jnp.moveaxis(parts, dim + level, 0)
        parts = direct_sum_scatter(parts, axis, stride, wires[level])
        stride *= splits[level]
    return parts


def butterfly_sum(array, axis):
    peers = lax.axis_size(axis)
    step = 1
    while step < peers:
        array = array + lax.ppermute(array, axis, [(i, i ^ step) for i in range(peers)])
        step *= 2
    return array


def side_by_side(arrays, axis, dim, along):
    widths = [a.shape[along] for a in arrays]
    both = jnp.concatenate(arrays, axis=along)
    filled = lax.psum_scatter(both, axis, scatter_dimension=dim, tiled=True)
    return tuple(jnp.split(filled, [sum(widths[:k]) for k in range(1, len(widths))], axis=along))


def bucket_slots(owners, capacity, peers):
    count = owners.shape[1]
    onehot = (owners[:, None, :] == jnp.arange(peers)[None, :, None]).astype(jnp.bfloat16)
    earlier = (jnp.arange(count)[:, None] < jnp.arange(count)[None, :]).astype(jnp.bfloat16)
    before = jnp.einsum("fpi,ij->fpj", onehot, earlier, preferred_element_type=jnp.float32)
    order_in = jnp.sum(before * onehot.astype(jnp.float32), axis=1)
    return owners * capacity + order_in.astype(jnp.int32)


def selection_matrix(indices, length):
    return (indices[:, :, None] == jnp.arange(length)[None, None, :]).astype(jnp.bfloat16)


def contract_last(left, right):
    return lax.dot_general(
        left, right, (((1,), (1,)), ((), ())), preferred_element_type=jnp.float32
    )


def contract_first(left, right):
    return lax.dot_general(
        left, right, (((0,), (0,)), ((), ())), preferred_element_type=jnp.float32
    )


def cross_down(state, v_layer):
    share = sum_at_owner(contract_last(state, v_layer), "mp", 0)
    return lax.all_gather(share.astype(jnp.bfloat16), "mp", axis=0, tiled=True)


def dp_factors(mesh):
    column = mesh.devices[:, 0]
    try:
        keys = [(d.coords[2], d.coords[0], d.core_on_chip) for d in column]
    except AttributeError:
        return (len(column),)
    factors = tuple(len(set(k[level] for k in keys)) for level in range(3))
    if int(np.prod(factors)) != len(column) or keys != sorted(keys):
        return (len(column),)
    return factors


def local(
    splits,
    embed_table,
    accum,
    stale_grad,
    grad_owner,
    grad_row,
    lookup_owner,
    lookup_row,
    bag_len,
    label,
    up_factor_weight,
    v_weight,
    cross_bias,
    head_weight,
):
    peers = lax.axis_size("dp")
    local_feats, grad_dev, width = stale_grad.shape
    rows_per_shard = embed_table.shape[1]
    which_feature = jnp.arange(local_feats)[:, None]
    grad_cap = max(2, 2 * grad_dev // peers)
    grad_total = peers * grad_cap
    grad_slot = bucket_slots(grad_owner[:, :, 0], grad_cap, peers)
    place = selection_matrix(grad_slot, grad_total)
    send_grads = jnp.einsum(
        "fns,fne->fse", place, stale_grad, preferred_element_type=jnp.float32
    ).astype(jnp.bfloat16)
    send_rows = (
        jnp.full((local_feats, grad_total), rows_per_shard, jnp.int32)
        .at[which_feature, grad_slot]
        .set(grad_row)
    )
    recv_grads = lax.all_to_all(
        send_grads.reshape(local_feats, peers, grad_cap, width),
        "dp",
        split_axis=1,
        concat_axis=1,
        tiled=True,
    )
    recv_rows = lax.all_to_all(
        send_rows.reshape(local_feats, peers, grad_cap),
        "dp",
        split_axis=1,
        concat_axis=1,
        tiled=True,
    )
    landing = selection_matrix(recv_rows.reshape(local_feats, grad_total), rows_per_shard)
    summed = jnp.einsum(
        "wjc,wjl->wcl",
        landing,
        recv_grads.reshape(local_feats, grad_total, width),
        preferred_element_type=jnp.float32,
    )
    new_accum = accum + jnp.mean(summed * summed, axis=2)
    new_table = embed_table - learn_rate * summed / jnp.sqrt(new_accum)[:, :, None]
    batch_dev = bag_len.shape[1]
    look_dev = lookup_row.shape[1]
    bag_size = look_dev // batch_dev
    look_cap = max(2, 2 * look_dev // peers)
    look_total = peers * look_cap
    look_slot = bucket_slots(lookup_owner[:, :, 0], look_cap, peers)
    wanted = (
        jnp.zeros((local_feats, look_total), jnp.int32).at[which_feature, look_slot].set(lookup_row)
    )
    requested_ids = lax.all_to_all(
        wanted.reshape(local_feats, peers, look_cap), "dp", split_axis=1, concat_axis=1, tiled=True
    ).reshape(local_feats, look_total)
    second_table = embed_table.astype(jnp.bfloat16)
    served = jnp.einsum(
        "adv,avm->adm",
        selection_matrix(requested_ids, rows_per_shard),
        second_table,
        preferred_element_type=jnp.float32,
    ).astype(jnp.bfloat16)
    returned = lax.all_to_all(
        served.reshape(local_feats, peers, look_cap, width),
        "dp",
        split_axis=1,
        concat_axis=1,
        tiled=True,
    ).reshape(local_feats, look_total, width)
    slots = look_slot.reshape(local_feats, batch_dev, bag_size)
    mixing = jnp.zeros((local_feats, batch_dev, look_total), jnp.bfloat16)
    for member in range(bag_size):
        used = (bag_len > member).astype(jnp.bfloat16)
        mixing = mixing + selection_matrix(slots[:, :, member], look_total) * used[:, :, None]
    pooled = jnp.einsum(
        "fbs,fse->fbe", mixing, returned, preferred_element_type=jnp.float32
    ).astype(jnp.bfloat16)
    start = jnp.transpose(pooled, (1, 0, 2)).reshape(batch_dev, local_feats * width)
    start_f = start.astype(jnp.float32)
    n_layers = up_factor_weight.shape[0]
    state = start
    states = []
    downs = []
    crosses = []
    for layer in range(n_layers):
        down_sum = cross_down(state, v_weight[layer])
        cross_out = (
            jnp.dot(down_sum, up_factor_weight[layer], preferred_element_type=jnp.float32)
            + cross_bias[layer]
        )
        states.append(state)
        downs.append(down_sum)
        crosses.append(cross_out)
        state = (start_f * cross_out + state.astype(jnp.float32)).astype(jnp.bfloat16)
    logit = lax.psum(jnp.sum(state.astype(jnp.float32) * head_weight[None, :], axis=1), "mp")
    slope = (jax.nn.sigmoid(logit) - label.astype(jnp.float32)) / jnp.sqrt(
        jnp.float32(batch_dev * peers)
    )
    upstream = slope[:, None] * head_weight[None, :]
    head_grad = jnp.sum(slope[:, None] * state.astype(jnp.float32), axis=0)
    to_start = jnp.zeros(start_f.shape, jnp.float32)
    grads_u = [None] * n_layers
    grads_v = [None] * n_layers
    bias_grads = [None] * n_layers
    for layer in reversed(range(n_layers)):
        direct = upstream * start_f
        bias_grads[layer] = jnp.sum(direct, axis=0)
        direct_bias_term = direct.astype(jnp.bfloat16)
        grad_u_layer = contract_first(downs[layer], direct_bias_term)
        back_sum = over_copies(
            contract_last(direct_bias_term, up_factor_weight[layer]), "mp"
        ).astype(jnp.bfloat16)
        down_factor_gradient = contract_first(back_sum, states[layer])
        to_start = to_start + upstream * crosses[layer]
        upstream = upstream + jnp.dot(back_sum, v_weight[layer], preferred_element_type=jnp.float32)
        grads_u[layer] = grad_u_layer
        grads_v[layer] = down_factor_gradient
    both = jnp.concatenate((jnp.stack(grads_u), jnp.stack(grads_v)), axis=0)
    wires = [jnp.float32] + [jnp.bfloat16] * (len(splits) - 1)
    grad_u, grad_v = jnp.split(tree_sum_scatter(both, "dp", 1, splits, wires), 2, axis=0)
    grad_small = butterfly_sum(jnp.stack(bias_grads + [head_grad]), "dp")
    grad_pooled = (upstream + to_start).astype(jnp.bfloat16)
    return (new_table, new_accum, grad_u, grad_v, grad_small, grad_pooled)


def solution(mesh):
    return jax.shard_map(
        functools.partial(local, dp_factors(mesh)),
        mesh=mesh,
        in_specs=(
            P("mp", "dp", None),
            P("mp", "dp"),
            P("mp", "dp", None),
            P("mp", "dp", None),
            P("mp", "dp"),
            P("mp", "dp", None),
            P("mp", "dp"),
            P("mp", "dp"),
            P("dp"),
            P(None, None, "mp"),
            P(None, None, "mp"),
            P(None, "mp"),
            P("mp"),
        ),
        out_specs=(
            P("mp", "dp", None),
            P("mp", "dp"),
            P(None, "dp", "mp"),
            P(None, "dp", "mp"),
            P(None, "mp"),
            P("dp", "mp"),
        ),
        check_vma=False,
    )
```

```python
import functools

import jax
import jax.numpy as jnp
import numpy as np
from jax import lax
from jax.sharding import PartitionSpec as P

learn_rate = 0.5


def in_blocks(array, dim, devices):
    shape = array.shape
    parts = array.reshape(*shape[:dim], devices, shape[dim] // devices, *shape[dim + 1 :])
    return jnp.moveaxis(parts, dim, 0)


def sum_at_owner(array, axis, dim):
    parts = in_blocks(array, dim, lax.axis_size(axis))
    arrived = lax.all_to_all(parts, axis, split_axis=0, concat_axis=0, tiled=True)
    return arrived.sum(axis=0)


def copy_for_each(array, axis):
    copies = jnp.broadcast_to(array, (lax.axis_size(axis), *array.shape))
    return lax.all_to_all(copies, axis, split_axis=0, concat_axis=0, tiled=True)


def over_copies(array, axis):
    return copy_for_each(array, axis).sum(axis=0)


def ring_sum_scatter(blocks, axis, stride, wire):
    size = blocks.shape[0]
    peers = lax.axis_size(axis)
    pos = (lax.axis_index(axis) // stride) % size
    ahead = [
        (i, i + (((i // stride) % size + 1) % size - (i // stride) % size) * stride)
        for i in range(peers)
    ]
    carry = blocks[(pos + size - 1) % size]
    for step in range(size - 1):
        arrived = lax.ppermute(carry.astype(wire), axis, ahead).astype(carry.dtype)
        carry = arrived + blocks[(pos + 2 * size - step - 2) % size]
    return carry

def direct_sum_scatter(blocks, axis, stride, wire):
    size = blocks.shape[0]
    peers = lax.axis_size(axis)
    pos = (lax.axis_index(axis) // stride) % size
    total = blocks[pos]
    for offset in range(1, size):
        toward = [
            (i, i + (((i // stride) % size + offset) % size - (i // stride) % size) * stride)
            for i in range(peers)
        ]
        sent = blocks[(pos + offset) % size].astype(wire)
        total = total + lax.ppermute(sent, axis, toward).astype(total.dtype)
    return total


def tree_sum_scatter(array, axis, dim, splits, wires):
    lead = array.shape[:dim]
    parts = array.reshape(*lead, *splits, array.shape[dim] // np.prod(splits), *array.shape[dim + 1:])
    stride = 1
    for level in reversed(range(len(splits))):
        parts = jnp.moveaxis(parts, dim + level, 0)
        parts = direct_sum_scatter(parts, axis, stride, wires[level])
        stride *= splits[level]
    return parts


def butterfly_sum(array, axis):
    peers = lax.axis_size(axis)
    step = 1
    while step < peers:
        array = array + lax.ppermute(array, axis, [(i, i ^ step) for i in range(peers)])
        step *= 2
    return array


def side_by_side(arrays, axis, dim, along):
    widths = [a.shape[along] for a in arrays]
    both = jnp.concatenate(arrays, axis=along)
    filled = lax.psum_scatter(both, axis, scatter_dimension=dim, tiled=True)
    return tuple(jnp.split(filled, [sum(widths[:k]) for k in range(1, len(widths))], axis=along))


def bucket_slots(owners, capacity, peers):
    count = owners.shape[1]
    onehot = (owners[:, None, :] == jnp.arange(peers)[None, :, None]).astype(jnp.bfloat16)
    earlier = (jnp.arange(count)[:, None] < jnp.arange(count)[None, :]).astype(jnp.bfloat16)
    before = jnp.einsum("fpi,ij->fpj", onehot, earlier, preferred_element_type=jnp.float32)
    order_in = jnp.sum(before * onehot.astype(jnp.float32), axis=1)
    return owners * capacity + order_in.astype(jnp.int32)


def selection_matrix(indices, length):
    return (indices[:, :, None] == jnp.arange(length)[None, None, :]).astype(jnp.bfloat16)


def contract_last(left, right):
    return lax.dot_general(
        left, right, (((1,), (1,)), ((), ())), preferred_element_type=jnp.float32
    )


def contract_first(left, right):
    return lax.dot_general(
        left, right, (((0,), (0,)), ((), ())), preferred_element_type=jnp.float32
    )


def cross_down(state, v_layer):
    share = sum_at_owner(contract_last(state, v_layer), "mp", 0)
    return lax.all_gather(share.astype(jnp.bfloat16), "mp", axis=0, tiled=True)


def dp_factors(mesh):
    column = mesh.devices[:, 0]
    try:
        keys = [(d.coords[2], d.coords[0], d.core_on_chip) for d in column]
    except AttributeError:
        return (len(column),)
    factors = tuple(len(set(k[level] for k in keys)) for level in range(3))
    if int(np.prod(factors)) != len(column) or keys != sorted(keys):
        return (len(column),)
    return factors


def local(
    splits,
    embed_table,
    accum,
    stale_grad,
    grad_owner,
    grad_row,
    lookup_owner,
    lookup_row,
    bag_len,
    label,
    up_factor_weight,
    v_weight,
    cross_bias,
    head_weight,
):
    peers = lax.axis_size("dp")
    local_feats, grad_dev, width = stale_grad.shape
    rows_per_shard = embed_table.shape[1]
    which_feature = jnp.arange(local_feats)[:, None]
    grad_cap = max(2, 2 * grad_dev // peers)
    grad_total = peers * grad_cap
    grad_slot = bucket_slots(grad_owner[:, :, 0], grad_cap, peers)
    place = selection_matrix(grad_slot, grad_total)
    send_grads = jnp.einsum(
        "fns,fne->fse", place, stale_grad, preferred_element_type=jnp.float32
    ).astype(jnp.bfloat16)
    send_rows = (
        jnp.full((local_feats, grad_total), rows_per_shard, jnp.int32)
        .at[which_feature, grad_slot]
        .set(grad_row)
    )
    recv_grads = lax.all_to_all(
        send_grads.reshape(local_feats, peers, grad_cap, width),
        "dp",
        split_axis=1,
        concat_axis=1,
        tiled=True,
    )
    recv_rows = lax.all_to_all(
        send_rows.reshape(local_feats, peers, grad_cap),
        "dp",
        split_axis=1,
        concat_axis=1,
        tiled=True,
    )
    landing = selection_matrix(recv_rows.reshape(local_feats, grad_total), rows_per_shard)
    summed = jnp.einsum(
        "wjc,wjl->wcl",
        landing,
        recv_grads.reshape(local_feats, grad_total, width),
        preferred_element_type=jnp.float32,
    )
    new_accum = accum + jnp.mean(summed * summed, axis=2)
    new_table = embed_table - learn_rate * summed / jnp.sqrt(new_accum)[:, :, None]
    batch_dev = bag_len.shape[1]
    look_dev = lookup_row.shape[1]
    bag_size = look_dev // batch_dev
    look_cap = max(2, 2 * look_dev // peers)
    look_total = peers * look_cap
    look_slot = bucket_slots(lookup_owner[:, :, 0], look_cap, peers)
    wanted = (
        jnp.zeros((local_feats, look_total), jnp.int32).at[which_feature, look_slot].set(lookup_row)
    )
    requested_ids = lax.all_to_all(
        wanted.reshape(local_feats, peers, look_cap), "dp", split_axis=1, concat_axis=1, tiled=True
    ).reshape(local_feats, look_total)
    second_table = embed_table.astype(jnp.bfloat16)
    served = jnp.einsum(
        "adv,avm->adm",
        selection_matrix(requested_ids, rows_per_shard),
        second_table,
        preferred_element_type=jnp.float32,
    ).astype(jnp.bfloat16)
    returned = lax.all_to_all(
        served.reshape(local_feats, peers, look_cap, width),
        "dp",
        split_axis=1,
        concat_axis=1,
        tiled=True,
    ).reshape(local_feats, look_total, width)
    slots = look_slot.reshape(local_feats, batch_dev, bag_size)
    mixing = jnp.zeros((local_feats, batch_dev, look_total), jnp.bfloat16)
    for member in range(bag_size):
        used = (bag_len > member).astype(jnp.bfloat16)
        mixing = mixing + selection_matrix(slots[:, :, member], look_total) * used[:, :, None]
    pooled = jnp.einsum(
        "fbs,fse->fbe", mixing, returned, preferred_element_type=jnp.float32
    ).astype(jnp.bfloat16)
    start = jnp.transpose(pooled, (1, 0, 2)).reshape(batch_dev, local_feats * width)
    start_f = start.astype(jnp.float32)
    n_layers = up_factor_weight.shape[0]
    state = start
    states = []
    downs = []
    crosses = []
    for layer in range(n_layers):
        down_sum = cross_down(state, v_weight[layer])
        cross_out = (
            jnp.dot(down_sum, up_factor_weight[layer], preferred_element_type=jnp.float32)
            + cross_bias[layer]
        )
        states.append(state)
        downs.append(down_sum)
        crosses.append(cross_out)
        state = (start_f * cross_out + state.astype(jnp.float32)).astype(jnp.bfloat16)
    logit = lax.psum(jnp.sum(state.astype(jnp.float32) * head_weight[None, :], axis=1), "mp")
    slope = (jax.nn.sigmoid(logit) - label.astype(jnp.float32)) / jnp.sqrt(
        jnp.float32(batch_dev * peers)
    )
    upstream = slope[:, None] * head_weight[None, :]
    head_grad = jnp.sum(slope[:, None] * state.astype(jnp.float32), axis=0)
    to_start = jnp.zeros(start_f.shape, jnp.float32)
    grads_u = [None] * n_layers
    grads_v = [None] * n_layers
    bias_grads = [None] * n_layers
    for layer in reversed(range(n_layers)):
        direct = upstream * start_f
        bias_grads[layer] = jnp.sum(direct, axis=0)
        direct_bias_term = direct.astype(jnp.bfloat16)
        grad_u_layer = contract_first(downs[layer], direct_bias_term)
        back_sum = over_copies(
            contract_last(direct_bias_term, up_factor_weight[layer]), "mp"
        ).astype(jnp.bfloat16)
        down_factor_gradient = contract_first(back_sum, states[layer])
        to_start = to_start + upstream * crosses[layer]
        upstream = upstream + jnp.dot(back_sum, v_weight[layer], preferred_element_type=jnp.float32)
        grads_u[layer] = grad_u_layer
        grads_v[layer] = down_factor_gradient
    both = jnp.concatenate((jnp.stack(grads_u), jnp.stack(grads_v)), axis=0)
    wires = [jnp.bfloat16] * len(splits)
    grad_u, grad_v = jnp.split(tree_sum_scatter(both, "dp", 1, splits, wires), 2, axis=0)
    grad_small = butterfly_sum(jnp.stack(bias_grads + [head_grad]), "dp")
    grad_pooled = (upstream + to_start).astype(jnp.bfloat16)
    return (new_table, new_accum, grad_u, grad_v, grad_small, grad_pooled)


def solution(mesh):
    return jax.shard_map(
        functools.partial(local, dp_factors(mesh)),
        mesh=mesh,
        in_specs=(
            P("mp", "dp", None),
            P("mp", "dp"),
            P("mp", "dp", None),
            P("mp", "dp", None),
            P("mp", "dp"),
            P("mp", "dp", None),
            P("mp", "dp"),
            P("mp", "dp"),
            P("dp"),
            P(None, None, "mp"),
            P(None, None, "mp"),
            P(None, "mp"),
            P("mp"),
        ),
        out_specs=(
            P("mp", "dp", None),
            P("mp", "dp"),
            P(None, "dp", "mp"),
            P(None, "dp", "mp"),
            P(None, "mp"),
            P("dp", "mp"),
        ),
        check_vma=False,
    )
```

```python
import functools

import jax
import jax.numpy as jnp
import numpy as np
from jax import lax
from jax.sharding import PartitionSpec as P

learn_rate = 0.5


def in_blocks(array, dim, devices):
    shape = array.shape
    parts = array.reshape(*shape[:dim], devices, shape[dim] // devices, *shape[dim + 1 :])
    return jnp.moveaxis(parts, dim, 0)


def sum_at_owner(array, axis, dim):
    parts = in_blocks(array, dim, lax.axis_size(axis))
    arrived = lax.all_to_all(parts, axis, split_axis=0, concat_axis=0, tiled=True)
    return arrived.sum(axis=0)


def copy_for_each(array, axis):
    copies = jnp.broadcast_to(array, (lax.axis_size(axis), *array.shape))
    return lax.all_to_all(copies, axis, split_axis=0, concat_axis=0, tiled=True)


def over_copies(array, axis):
    return copy_for_each(array, axis).sum(axis=0)


def ring_sum_scatter(blocks, axis, stride, wire):
    size = blocks.shape[0]
    peers = lax.axis_size(axis)
    pos = (lax.axis_index(axis) // stride) % size
    ahead = [
        (i, i + (((i // stride) % size + 1) % size - (i // stride) % size) * stride)
        for i in range(peers)
    ]
    carry = blocks[(pos + size - 1) % size]
    for step in range(size - 1):
        arrived = lax.ppermute(carry.astype(wire), axis, ahead).astype(carry.dtype)
        carry = arrived + blocks[(pos + 2 * size - step - 2) % size]
    return carry

def direct_sum_scatter(blocks, axis, stride, wire):
    size = blocks.shape[0]
    peers = lax.axis_size(axis)
    pos = (lax.axis_index(axis) // stride) % size
    total = blocks[pos]
    for offset in range(1, size):
        toward = [
            (i, i + (((i // stride) % size + offset) % size - (i // stride) % size) * stride)
            for i in range(peers)
        ]
        sent = blocks[(pos + offset) % size].astype(wire)
        total = total + lax.ppermute(sent, axis, toward).astype(total.dtype)
    return total


def tree_sum_scatter(array, axis, dim, splits, wires):
    lead = array.shape[:dim]
    parts = array.reshape(*lead, *splits, array.shape[dim] // np.prod(splits), *array.shape[dim + 1:])
    stride = 1
    for level in reversed(range(len(splits))):
        parts = jnp.moveaxis(parts, dim + level, 0)
        parts = direct_sum_scatter(parts, axis, stride, wires[level])
        stride *= splits[level]
    return parts


def butterfly_sum(array, axis):
    peers = lax.axis_size(axis)
    step = 1
    while step < peers:
        array = array + lax.ppermute(array, axis, [(i, i ^ step) for i in range(peers)])
        step *= 2
    return array


def side_by_side(arrays, axis, dim, along):
    widths = [a.shape[along] for a in arrays]
    both = jnp.concatenate(arrays, axis=along)
    filled = lax.psum_scatter(both, axis, scatter_dimension=dim, tiled=True)
    return tuple(jnp.split(filled, [sum(widths[:k]) for k in range(1, len(widths))], axis=along))


def bucket_slots(owners, capacity, peers):
    count = owners.shape[1]
    onehot = (owners[:, None, :] == jnp.arange(peers)[None, :, None]).astype(jnp.bfloat16)
    earlier = (jnp.arange(count)[:, None] < jnp.arange(count)[None, :]).astype(jnp.bfloat16)
    before = jnp.einsum("fpi,ij->fpj", onehot, earlier, preferred_element_type=jnp.float32)
    order_in = jnp.sum(before * onehot.astype(jnp.float32), axis=1)
    return owners * capacity + order_in.astype(jnp.int32)


def selection_matrix(indices, length):
    return (indices[:, :, None] == jnp.arange(length)[None, None, :]).astype(jnp.bfloat16)


def contract_last(left, right):
    return lax.dot_general(
        left, right, (((1,), (1,)), ((), ())), preferred_element_type=jnp.float32
    )


def contract_first(left, right):
    return lax.dot_general(
        left, right, (((0,), (0,)), ((), ())), preferred_element_type=jnp.float32
    )


def cross_down(state, v_layer):
    share = sum_at_owner(contract_last(state, v_layer), "mp", 0)
    return lax.all_gather(share.astype(jnp.bfloat16), "mp", axis=0, tiled=True)


def dp_factors(mesh):
    column = mesh.devices[:, 0]
    try:
        keys = [(d.coords[2], d.coords[0], d.core_on_chip) for d in column]
    except AttributeError:
        return (len(column),)
    factors = tuple(len(set(k[level] for k in keys)) for level in range(3))
    if int(np.prod(factors)) != len(column) or keys != sorted(keys):
        return (len(column),)
    return factors


def local(
    splits,
    embed_table,
    accum,
    stale_grad,
    grad_owner,
    grad_row,
    lookup_owner,
    lookup_row,
    bag_len,
    label,
    up_factor_weight,
    v_weight,
    cross_bias,
    head_weight,
):
    peers = lax.axis_size("dp")
    local_feats, grad_dev, width = stale_grad.shape
    rows_per_shard = embed_table.shape[1]
    which_feature = jnp.arange(local_feats)[:, None]
    grad_cap = max(2, 2 * grad_dev // peers)
    grad_total = peers * grad_cap
    grad_slot = bucket_slots(grad_owner[:, :, 0], grad_cap, peers)
    place = selection_matrix(grad_slot, grad_total)
    send_grads = jnp.einsum(
        "fns,fne->fse", place, stale_grad, preferred_element_type=jnp.float32
    ).astype(jnp.bfloat16)
    send_rows = (
        jnp.full((local_feats, grad_total), rows_per_shard, jnp.int32)
        .at[which_feature, grad_slot]
        .set(grad_row)
    )
    recv_grads = jnp.concatenate(
        [
            lax.all_to_all(half, "dp", split_axis=1, concat_axis=1, tiled=True)
            for half in jnp.split(send_grads.reshape(local_feats, peers, grad_cap, width), 2, axis=0)
        ],
        axis=0,
    )
    recv_rows = lax.all_to_all(
        send_rows.reshape(local_feats, peers, grad_cap),
        "dp",
        split_axis=1,
        concat_axis=1,
        tiled=True,
    )
    landing = selection_matrix(recv_rows.reshape(local_feats, grad_total), rows_per_shard)
    summed = jnp.einsum(
        "wjc,wjl->wcl",
        landing,
        recv_grads.reshape(local_feats, grad_total, width),
        preferred_element_type=jnp.float32,
    )
    new_accum = accum + jnp.mean(summed * summed, axis=2)
    new_table = embed_table - learn_rate * summed / jnp.sqrt(new_accum)[:, :, None]
    batch_dev = bag_len.shape[1]
    look_dev = lookup_row.shape[1]
    bag_size = look_dev // batch_dev
    look_cap = max(2, 2 * look_dev // peers)
    look_total = peers * look_cap
    look_slot = bucket_slots(lookup_owner[:, :, 0], look_cap, peers)
    wanted = (
        jnp.zeros((local_feats, look_total), jnp.int32).at[which_feature, look_slot].set(lookup_row)
    )
    requested_ids = lax.all_to_all(
        wanted.reshape(local_feats, peers, look_cap), "dp", split_axis=1, concat_axis=1, tiled=True
    ).reshape(local_feats, look_total)
    second_table = embed_table.astype(jnp.bfloat16)
    served = jnp.einsum(
        "adv,avm->adm",
        selection_matrix(requested_ids, rows_per_shard),
        second_table,
        preferred_element_type=jnp.float32,
    ).astype(jnp.bfloat16)
    returned = lax.all_to_all(
        served.reshape(local_feats, peers, look_cap, width),
        "dp",
        split_axis=1,
        concat_axis=1,
        tiled=True,
    ).reshape(local_feats, look_total, width)
    slots = look_slot.reshape(local_feats, batch_dev, bag_size)
    mixing = jnp.zeros((local_feats, batch_dev, look_total), jnp.bfloat16)
    for member in range(bag_size):
        used = (bag_len > member).astype(jnp.bfloat16)
        mixing = mixing + selection_matrix(slots[:, :, member], look_total) * used[:, :, None]
    pooled = jnp.einsum(
        "fbs,fse->fbe", mixing, returned, preferred_element_type=jnp.float32
    ).astype(jnp.bfloat16)
    start = jnp.transpose(pooled, (1, 0, 2)).reshape(batch_dev, local_feats * width)
    start_f = start.astype(jnp.float32)
    n_layers = up_factor_weight.shape[0]
    state = start
    states = []
    downs = []
    crosses = []
    for layer in range(n_layers):
        down_sum = cross_down(state, v_weight[layer])
        cross_out = (
            jnp.dot(down_sum, up_factor_weight[layer], preferred_element_type=jnp.float32)
            + cross_bias[layer]
        )
        states.append(state)
        downs.append(down_sum)
        crosses.append(cross_out)
        state = (start_f * cross_out + state.astype(jnp.float32)).astype(jnp.bfloat16)
    logit = lax.psum(jnp.sum(state.astype(jnp.float32) * head_weight[None, :], axis=1), "mp")
    slope = (jax.nn.sigmoid(logit) - label.astype(jnp.float32)) / jnp.sqrt(
        jnp.float32(batch_dev * peers)
    )
    upstream = slope[:, None] * head_weight[None, :]
    head_grad = jnp.sum(slope[:, None] * state.astype(jnp.float32), axis=0)
    to_start = jnp.zeros(start_f.shape, jnp.float32)
    grads_u = [None] * n_layers
    grads_v = [None] * n_layers
    bias_grads = [None] * n_layers
    for layer in reversed(range(n_layers)):
        direct = upstream * start_f
        bias_grads[layer] = jnp.sum(direct, axis=0)
        direct_bias_term = direct.astype(jnp.bfloat16)
        grad_u_layer = contract_first(downs[layer], direct_bias_term)
        back_sum = over_copies(
            contract_last(direct_bias_term, up_factor_weight[layer]), "mp"
        ).astype(jnp.bfloat16)
        down_factor_gradient = contract_first(back_sum, states[layer])
        to_start = to_start + upstream * crosses[layer]
        upstream = upstream + jnp.dot(back_sum, v_weight[layer], preferred_element_type=jnp.float32)
        grads_u[layer] = grad_u_layer
        grads_v[layer] = down_factor_gradient
    both = jnp.concatenate((jnp.stack(grads_u), jnp.stack(grads_v)), axis=0)
    wires = [jnp.bfloat16] * len(splits)
    grad_u, grad_v = jnp.split(tree_sum_scatter(both, "dp", 1, splits, wires), 2, axis=0)
    grad_small = butterfly_sum(jnp.stack(bias_grads + [head_grad]), "dp")
    grad_pooled = (upstream + to_start).astype(jnp.bfloat16)
    return (new_table, new_accum, grad_u, grad_v, grad_small, grad_pooled)


def solution(mesh):
    return jax.shard_map(
        functools.partial(local, dp_factors(mesh)),
        mesh=mesh,
        in_specs=(
            P("mp", "dp", None),
            P("mp", "dp"),
            P("mp", "dp", None),
            P("mp", "dp", None),
            P("mp", "dp"),
            P("mp", "dp", None),
            P("mp", "dp"),
            P("mp", "dp"),
            P("dp"),
            P(None, None, "mp"),
            P(None, None, "mp"),
            P(None, "mp"),
            P("mp"),
        ),
        out_specs=(
            P("mp", "dp", None),
            P("mp", "dp"),
            P(None, "dp", "mp"),
            P(None, "dp", "mp"),
            P(None, "mp"),
            P("dp", "mp"),
        ),
        check_vma=False,
    )
```

```python
import functools

import jax
import jax.numpy as jnp
import numpy as np
from jax import lax
from jax.sharding import PartitionSpec as P

learn_rate = 0.5


def in_blocks(array, dim, devices):
    shape = array.shape
    parts = array.reshape(*shape[:dim], devices, shape[dim] // devices, *shape[dim + 1 :])
    return jnp.moveaxis(parts, dim, 0)


def sum_at_owner(array, axis, dim):
    parts = in_blocks(array, dim, lax.axis_size(axis))
    arrived = lax.all_to_all(parts, axis, split_axis=0, concat_axis=0, tiled=True)
    return arrived.sum(axis=0)


def copy_for_each(array, axis):
    copies = jnp.broadcast_to(array, (lax.axis_size(axis), *array.shape))
    return lax.all_to_all(copies, axis, split_axis=0, concat_axis=0, tiled=True)


def over_copies(array, axis):
    return copy_for_each(array, axis).sum(axis=0)


def ring_sum_scatter(blocks, axis, stride, wire):
    size = blocks.shape[0]
    peers = lax.axis_size(axis)
    pos = (lax.axis_index(axis) // stride) % size
    ahead = [
        (i, i + (((i // stride) % size + 1) % size - (i // stride) % size) * stride)
        for i in range(peers)
    ]
    carry = blocks[(pos + size - 1) % size]
    for step in range(size - 1):
        arrived = lax.ppermute(carry.astype(wire), axis, ahead).astype(carry.dtype)
        carry = arrived + blocks[(pos + 2 * size - step - 2) % size]
    return carry

def direct_sum_scatter(blocks, axis, stride, wire):
    size = blocks.shape[0]
    peers = lax.axis_size(axis)
    pos = (lax.axis_index(axis) // stride) % size
    total = blocks[pos]
    for offset in range(1, size):
        toward = [
            (i, i + (((i // stride) % size + offset) % size - (i // stride) % size) * stride)
            for i in range(peers)
        ]
        sent = blocks[(pos + offset) % size].astype(wire)
        total = total + lax.ppermute(sent, axis, toward).astype(total.dtype)
    return total


def tree_sum_scatter(array, axis, dim, splits, wires):
    lead = array.shape[:dim]
    parts = array.reshape(*lead, *splits, array.shape[dim] // np.prod(splits), *array.shape[dim + 1:])
    stride = 1
    for level in reversed(range(len(splits))):
        parts = jnp.moveaxis(parts, dim + level, 0)
        parts = direct_sum_scatter(parts, axis, stride, wires[level])
        stride *= splits[level]
    return parts


def butterfly_sum(array, axis):
    peers = lax.axis_size(axis)
    step = 1
    while step < peers:
        array = array + lax.ppermute(array, axis, [(i, i ^ step) for i in range(peers)])
        step *= 2
    return array


def side_by_side(arrays, axis, dim, along):
    widths = [a.shape[along] for a in arrays]
    both = jnp.concatenate(arrays, axis=along)
    filled = lax.psum_scatter(both, axis, scatter_dimension=dim, tiled=True)
    return tuple(jnp.split(filled, [sum(widths[:k]) for k in range(1, len(widths))], axis=along))


def bucket_slots(owners, capacity, peers):
    count = owners.shape[1]
    onehot = (owners[:, None, :] == jnp.arange(peers)[None, :, None]).astype(jnp.bfloat16)
    earlier = (jnp.arange(count)[:, None] < jnp.arange(count)[None, :]).astype(jnp.bfloat16)
    before = jnp.einsum("fpi,ij->fpj", onehot, earlier, preferred_element_type=jnp.float32)
    order_in = jnp.sum(before * onehot.astype(jnp.float32), axis=1)
    return owners * capacity + order_in.astype(jnp.int32)


def selection_matrix(indices, length):
    return (indices[:, :, None] == jnp.arange(length)[None, None, :]).astype(jnp.bfloat16)


def placed_ints(onehot, values):
    digits = jnp.stack((values // 32, values % 32), axis=-1).astype(jnp.bfloat16)
    moved = jnp.einsum("fns,fnk->fsk", onehot, digits, preferred_element_type=jnp.float32)
    return moved[..., 0].astype(jnp.int32) * 32 + moved[..., 1].astype(jnp.int32)


def contract_last(left, right):
    return lax.dot_general(
        left, right, (((1,), (1,)), ((), ())), preferred_element_type=jnp.float32
    )


def contract_first(left, right):
    return lax.dot_general(
        left, right, (((0,), (0,)), ((), ())), preferred_element_type=jnp.float32
    )


def cross_down(state, v_layer):
    share = sum_at_owner(contract_last(state, v_layer), "mp", 0)
    return lax.all_gather(share.astype(jnp.bfloat16), "mp", axis=0, tiled=True)


def dp_factors(mesh):
    column = mesh.devices[:, 0]
    try:
        keys = [(d.coords[2], d.coords[0], d.core_on_chip) for d in column]
    except AttributeError:
        return (len(column),)
    factors = tuple(len(set(k[level] for k in keys)) for level in range(3))
    if int(np.prod(factors)) != len(column) or keys != sorted(keys):
        return (len(column),)
    return factors


def local(
    splits,
    embed_table,
    accum,
    stale_grad,
    grad_owner,
    grad_row,
    lookup_owner,
    lookup_row,
    bag_len,
    label,
    up_factor_weight,
    v_weight,
    cross_bias,
    head_weight,
):
    peers = lax.axis_size("dp")
    local_feats, grad_dev, width = stale_grad.shape
    rows_per_shard = embed_table.shape[1]
    which_feature = jnp.arange(local_feats)[:, None]
    grad_cap = max(2, 2 * grad_dev // peers)
    grad_total = peers * grad_cap
    grad_slot = bucket_slots(grad_owner[:, :, 0], grad_cap, peers)
    place = selection_matrix(grad_slot, grad_total)
    send_grads = jnp.einsum(
        "fns,fne->fse", place, stale_grad, preferred_element_type=jnp.float32
    ).astype(jnp.bfloat16)
    send_rows = placed_ints(place, grad_row + 1) - 1
    recv_grads = lax.all_to_all(
        send_grads.reshape(local_feats, peers, grad_cap, width),
        "dp",
        split_axis=1,
        concat_axis=1,
        tiled=True,
    )
    recv_rows = lax.all_to_all(
        send_rows.reshape(local_feats, peers, grad_cap),
        "dp",
        split_axis=1,
        concat_axis=1,
        tiled=True,
    )
    landing = selection_matrix(recv_rows.reshape(local_feats, grad_total), rows_per_shard)
    summed = jnp.einsum(
        "wjc,wjl->wcl",
        landing,
        recv_grads.reshape(local_feats, grad_total, width),
        preferred_element_type=jnp.float32,
    )
    new_accum = accum + jnp.mean(summed * summed, axis=2)
    new_table = embed_table - learn_rate * summed / jnp.sqrt(new_accum)[:, :, None]
    batch_dev = bag_len.shape[1]
    look_dev = lookup_row.shape[1]
    bag_size = look_dev // batch_dev
    look_cap = max(2, 2 * look_dev // peers)
    look_total = peers * look_cap
    look_slot = bucket_slots(lookup_owner[:, :, 0], look_cap, peers)
    wanted = placed_ints(selection_matrix(look_slot, look_total), lookup_row)
    requested_ids = lax.all_to_all(
        wanted.reshape(local_feats, peers, look_cap), "dp", split_axis=1, concat_axis=1, tiled=True
    ).reshape(local_feats, look_total)
    second_table = embed_table.astype(jnp.bfloat16)
    served = jnp.einsum(
        "adv,avm->adm",
        selection_matrix(requested_ids, rows_per_shard),
        second_table,
        preferred_element_type=jnp.float32,
    ).astype(jnp.bfloat16)
    returned = lax.all_to_all(
        served.reshape(local_feats, peers, look_cap, width),
        "dp",
        split_axis=1,
        concat_axis=1,
        tiled=True,
    ).reshape(local_feats, look_total, width)
    slots = look_slot.reshape(local_feats, batch_dev, bag_size)
    mixing = jnp.zeros((local_feats, batch_dev, look_total), jnp.bfloat16)
    for member in range(bag_size):
        used = (bag_len > member).astype(jnp.bfloat16)
        mixing = mixing + selection_matrix(slots[:, :, member], look_total) * used[:, :, None]
    pooled = jnp.einsum(
        "fbs,fse->fbe", mixing, returned, preferred_element_type=jnp.float32
    ).astype(jnp.bfloat16)
    start = jnp.transpose(pooled, (1, 0, 2)).reshape(batch_dev, local_feats * width)
    start_f = start.astype(jnp.float32)
    n_layers = up_factor_weight.shape[0]
    state = start
    states = []
    downs = []
    crosses = []
    for layer in range(n_layers):
        down_sum = cross_down(state, v_weight[layer])
        cross_out = (
            jnp.dot(down_sum, up_factor_weight[layer], preferred_element_type=jnp.float32)
            + cross_bias[layer]
        )
        states.append(state)
        downs.append(down_sum)
        crosses.append(cross_out)
        state = (start_f * cross_out + state.astype(jnp.float32)).astype(jnp.bfloat16)
    logit = lax.psum(jnp.sum(state.astype(jnp.float32) * head_weight[None, :], axis=1), "mp")
    slope = (jax.nn.sigmoid(logit) - label.astype(jnp.float32)) / jnp.sqrt(
        jnp.float32(batch_dev * peers)
    )
    upstream = slope[:, None] * head_weight[None, :]
    head_grad = jnp.sum(slope[:, None] * state.astype(jnp.float32), axis=0)
    to_start = jnp.zeros(start_f.shape, jnp.float32)
    grads_u = [None] * n_layers
    grads_v = [None] * n_layers
    bias_grads = [None] * n_layers
    for layer in reversed(range(n_layers)):
        direct = upstream * start_f
        bias_grads[layer] = jnp.sum(direct, axis=0)
        direct_bias_term = direct.astype(jnp.bfloat16)
        grad_u_layer = contract_first(downs[layer], direct_bias_term)
        back_sum = over_copies(
            contract_last(direct_bias_term, up_factor_weight[layer]), "mp"
        ).astype(jnp.bfloat16)
        down_factor_gradient = contract_first(back_sum, states[layer])
        to_start = to_start + upstream * crosses[layer]
        upstream = upstream + jnp.dot(back_sum, v_weight[layer], preferred_element_type=jnp.float32)
        grads_u[layer] = grad_u_layer
        grads_v[layer] = down_factor_gradient
    both = jnp.concatenate((jnp.stack(grads_u), jnp.stack(grads_v)), axis=0)
    wires = [jnp.bfloat16] * len(splits)
    grad_u, grad_v = jnp.split(tree_sum_scatter(both, "dp", 1, splits, wires), 2, axis=0)
    grad_small = butterfly_sum(jnp.stack(bias_grads + [head_grad]), "dp")
    grad_pooled = (upstream + to_start).astype(jnp.bfloat16)
    return (new_table, new_accum, grad_u, grad_v, grad_small, grad_pooled)


def solution(mesh):
    return jax.shard_map(
        functools.partial(local, dp_factors(mesh)),
        mesh=mesh,
        in_specs=(
            P("mp", "dp", None),
            P("mp", "dp"),
            P("mp", "dp", None),
            P("mp", "dp", None),
            P("mp", "dp"),
            P("mp", "dp", None),
            P("mp", "dp"),
            P("mp", "dp"),
            P("dp"),
            P(None, None, "mp"),
            P(None, None, "mp"),
            P(None, "mp"),
            P("mp"),
        ),
        out_specs=(
            P("mp", "dp", None),
            P("mp", "dp"),
            P(None, "dp", "mp"),
            P(None, "dp", "mp"),
            P(None, "mp"),
            P("dp", "mp"),
        ),
        check_vma=False,
    )
```
